512 devices in a mesh: ctx: 64 (over z_hi, y, x), ch: 8 (over z_lo, core).
Axes of the slice: x: 4, y: 4, z: 16 (z_hi: 4, z_lo: 4; z = z_hi * 4 + z_lo), core: 2. Of those that a mesh axis runs over, the one named last changes fastest.
Arguments:
- first_gate: bfloat16 [8192, 8192], P('ctx', 'ch'), may hold values from -6 to 6
- second_gate: bfloat16 [8192, 8192], P('ctx', 'ch'), may hold values from -6 to 6
- output_gate: bfloat16 [8192, 8192], P('ctx', 'ch'), may hold values from -6 to 6
- values: bfloat16 [8192, 8192], P('ctx', 'ch'), may hold values from -6 to 6
- cotangent: bfloat16 [8192, 8192], P('ctx', 'ch'), may hold values from -6 to 6
- medium_filter: bfloat16 [128, 512], P(None, 'ch'), may hold values from -0.5 to 0.5
- long_filter: bfloat16 [8192, 512], P('ctx', 'ch'), may hold values from -0.044194174 to 0.044194174
Outputs:
- grad_first: bfloat16 [8192, 8192], P('ctx', 'ch')
- grad_second: bfloat16 [8192, 8192], P('ctx', 'ch')
- grad_output_gate: bfloat16 [8192, 8192], P('ctx', 'ch')
- grad_values: bfloat16 [8192, 8192], P('ctx', 'ch')
- grad_medium: float32 [128, 512], P(None, 'ch')
- grad_long: bfloat16 [8192, 512], P('ctx', 'ch')
- filter_rms: float32 [], replicated
The draws below stay inside these ranges and needn't reach their ends.
All inputs are finite; a program needn't handle non-finite values.
Results may differ from the reference program's by a relative error of at most 0.011.
Values may be sent and summed in bfloat16 or wider, within the bound.
No kernel may reach another device: no remote copies, remote signals or barrier semaphores. Data moves between devices by JAX's collectives and lax.ppermute only.
A program may use at most 64 MiB of HBM per device.

```python
import math
import jax
import jax.numpy as jnp
from jax import lax

D = 8192
TAPS = 128
GROUP = 16
TOKENS = 8192
GROUPS = 512
N_CH = 8


def draw_long_filter(key, part):
    noise_key, rate_key = jax.random.split(jax.random.fold_in(key, 17))
    group_count = D // GROUP
    positions = jnp.arange(TOKENS, dtype=jnp.float32)[:, None]
    noise = jnp.clip(jax.random.normal(noise_key, (TOKENS, group_count), jnp.float32), -4.0, 4.0)
    rates = jnp.exp(jax.random.uniform(rate_key, (1, group_count), jnp.float32, math.log(0.5), math.log(40.0)))
    filt = noise * jnp.exp(-rates * positions / TOKENS) / math.sqrt(TOKENS)
    return filt.astype(jnp.bfloat16)


def block_scale(stream_key, extent, cuts, least, top_value):
    def one(position, shards_of):
        steps = jax.random.uniform(jax.random.fold_in(jax.random.fold_in(stream_key, 6), position), (shards_of,), jnp.float32, least / len(cuts), top_value / len(cuts))
        return jnp.repeat(jnp.exp(steps), extent[position] // shards_of).reshape((-1,) + (1,) * (len(extent) - position - 1))

    level = one(*cuts[0])
    for cut in cuts[1:]:
        level = level * one(*cut)
    return level


def bell_draw(key, extent, width, reach, shards=(), kind=jnp.bfloat16):
    drawn = jax.random.normal(key, extent, jnp.float32) * width
    if len(shards) > 0:
        drawn = block_scale(key, extent, shards, -0.22, 0.18) * drawn
    return jnp.clip(drawn, min=-reach, max=reach).astype(kind)


def setup_inputs(seed: int = 0) -> dict:
    keys = jax.random.split(jax.random.key(seed), 8)
    first_gate = bell_draw(keys[0], (TOKENS, D), 1.0, 6.0, ((0, 64), (1, 8)))
    second_gate = bell_draw(keys[1], (TOKENS, D), 1.0, 6.0, ((0, 64), (1, 8)))
    output_gate = bell_draw(keys[2], (TOKENS, D), 1.0, 6.0, ((0, 64), (1, 8)))
    values = bell_draw(keys[3], (TOKENS, D), 1.0, 6.0, ((0, 64), (1, 8)))
    cotangent = bell_draw(keys[4], (TOKENS, D), 1.0, 6.0, ((0, 64), (1, 8)))
    medium_filter = bell_draw(keys[5], (TAPS, GROUPS), TAPS ** -0.5, 0.5, ((1, 8),))
    long_filter = draw_long_filter(jax.random.fold_in(keys[7], 71), 0)
    return {"first_gate": first_gate, "second_gate": second_gate, "output_gate": output_gate, "values": values, "cotangent": cotangent, "medium_filter": medium_filter, "long_filter": long_filter}


def rounded(value):
    return lax.optimization_barrier(value.astype(jnp.bfloat16)).astype(jnp.float32)

def reference(first_gate, second_gate, output_gate, values, cotangent, medium_filter, long_filter):
    seq_len, model_width = first_gate.shape
    tap_count, group_total = medium_filter.shape
    group_size = model_width // group_total
    block_total = N_CH
    block_width = model_width // block_total
    block_groups = group_total // block_total
    scale = 1.0 / math.sqrt(seq_len * group_size)
    fft_len = 2 * seq_len

    def by_block(matrix):
        return matrix.reshape(matrix.shape[0], block_total, -1).transpose(1, 0, 2)

    def unblock(stacked):
        return stacked.transpose(1, 0, 2).reshape(stacked.shape[1], -1)

    def one_block(operands):
        gate_one, gate_two, gate_three, value_part, grad_part, medium_part, long_part = operands
        gate_one = gate_one.astype(jnp.float32)
        gate_two = gate_two.astype(jnp.float32)
        gate_three = gate_three.astype(jnp.float32)
        value_part = value_part.astype(jnp.float32)
        grad_part = grad_part.astype(jnp.float32)
        medium_wide = jnp.repeat(medium_part.astype(jnp.float32), group_size, axis=1)
        gated = rounded(gate_one * value_part)
        padded_gate = jnp.concatenate([jnp.zeros((tap_count - 1, block_width), jnp.float32), gated], axis=0)

        def forward_tap(tap, total):
            start = (tap_count - 1 - tap).astype(jnp.int32)
            return total + medium_wide[tap] * lax.dynamic_slice_in_dim(padded_gate, start, seq_len, 0)
        mixed = lax.fori_loop(0, tap_count, forward_tap, jnp.zeros((seq_len, block_width), jnp.float32))
        carried = rounded(gate_two * mixed)
        inner = rounded(grad_part * gate_three)
        long_spec = jnp.fft.rfft(long_part.astype(jnp.float32), n=fft_len, axis=0)
        long_wide = jnp.repeat(long_spec, group_size, axis=1)
        carried_spec = jnp.fft.rfft(carried, n=fft_len, axis=0)
        inner_spec = jnp.fft.rfft(inner, n=fft_len, axis=0)
        second = rounded(jnp.fft.irfft(carried_spec * long_wide, n=fft_len, axis=0)[:seq_len])
        grad_carried = rounded(jnp.fft.irfft(inner_spec * jnp.conj(long_wide), n=fft_len, axis=0)[:seq_len])
        corr_spec = (inner_spec * jnp.conj(carried_spec)).reshape(-1, block_groups, group_size).sum(axis=2)
        grad_long = (jnp.fft.irfft(corr_spec, n=fft_len, axis=0)[:seq_len] * scale).astype(jnp.bfloat16)
        grad_output_gate = (grad_part * second).astype(jnp.bfloat16)
        grad_second = (grad_carried * mixed).astype(jnp.bfloat16)
        grad_mixed = rounded(grad_carried * gate_two)
        trailing = jnp.concatenate([grad_mixed, jnp.zeros((tap_count - 1, block_width), jnp.float32)], axis=0)

        def backward_tap(tap, total):
            start = jnp.asarray(tap).astype(jnp.int32)
            return total + medium_wide[tap] * lax.dynamic_slice_in_dim(trailing, start, seq_len, 0)
        grad_gated = lax.fori_loop(0, tap_count, backward_tap, jnp.zeros((seq_len, block_width), jnp.float32))
        grad_first = (grad_gated * value_part).astype(jnp.bfloat16)
        grad_values = (grad_gated * gate_one).astype(jnp.bfloat16)

        def medium_lag(tap):
            start = (tap_count - 1 - tap).astype(jnp.int32)
            shifted = lax.dynamic_slice_in_dim(padded_gate, start, seq_len, 0)
            return lax.optimization_barrier(jnp.sum((grad_mixed * shifted).reshape(seq_len, block_groups, group_size), axis=(0, 2))) * scale
        grad_medium = lax.map(medium_lag, jnp.arange(tap_count, dtype=jnp.int32))
        return (grad_first, grad_second, grad_output_gate, grad_values, grad_medium, grad_long)
    stacked = (by_block(first_gate), by_block(second_gate), by_block(output_gate), by_block(values), by_block(cotangent), by_block(medium_filter), by_block(long_filter))
    results = lax.map(one_block, stacked)
    grad_first = unblock(results[0])
    grad_second = unblock(results[1])
    grad_output_gate = unblock(results[2])
    grad_values = unblock(results[3])
    grad_medium = unblock(results[4])
    grad_long = unblock(results[5])
    squares = jnp.sum(jnp.square(grad_long.astype(jnp.float32))) + jnp.sum(jnp.square(grad_medium))
    filter_rms = jnp.sqrt(squares / ((seq_len + tap_count) * group_total))
    return (grad_first, grad_second, grad_output_gate, grad_values, grad_medium, grad_long, filter_rms)
```

```python
import math

import jax
import jax.numpy as jnp
from jax import lax
from jax.sharding import PartitionSpec as P

radix_cols = 128
block_limit = 64
highest = lax.Precision.HIGHEST
wide_type = jnp.float32
narrow_type = jnp.bfloat16


def passed_along(array, axis, by):
    peers = lax.axis_size(axis)
    pairs = [(i, i + by) for i in range(peers) if 0 <= i + by < peers]
    return lax.ppermute(array, axis, pairs)


def band_table(filt, block_rows, flipped):
    tap_count, group_count = filt.shape
    window_rows = block_rows + tap_count - 1
    leading = filt[::-1] if flipped else filt
    padded = jnp.concatenate([leading.T, jnp.zeros((group_count, block_rows), filt.dtype)], axis=1)
    tiled = jnp.broadcast_to(padded[:, None, :], (group_count, block_rows, window_rows + 1))
    tiled = tiled.reshape(group_count, block_rows * (window_rows + 1))
    return tiled[:, : block_rows * window_rows].reshape(group_count, block_rows, window_rows)


def windows_of(extended, block_rows, block_count, window_rows):
    return jnp.stack(
        [
            extended[number * block_rows : number * block_rows + window_rows]
            for number in range(block_count)
        ]
    )


def phase_table(row_count, col_count, period):
    row_ids = lax.broadcasted_iota(jnp.int32, (row_count, col_count), 0)
    col_ids = lax.broadcasted_iota(jnp.int32, (row_count, col_count), 1)
    angle = (row_ids * col_ids % period).astype(wide_type) * (2.0 * math.pi / period)
    return (jnp.cos(angle), jnp.sin(angle))


def forward_dft(signal, tables):
    outer_table, cos_twist, sin_twist, forward_inner, inverse_inner = tables
    outer = jnp.einsum("kna,nmb->mkab", outer_table, signal, precision=highest)
    real_part = outer[:, 0]
    imag_part = outer[:, 1]
    twisted = jnp.stack(
        [
            real_part * cos_twist + imag_part * sin_twist,
            imag_part * cos_twist - real_part * sin_twist,
        ],
        axis=1,
    )
    return jnp.einsum("mkab,kjbq->mjaq", twisted, forward_inner, precision=highest)


def inverse_dft(spectrum, tables, total_len):
    outer_table, cos_twist, sin_twist, forward_inner, inverse_inner = tables
    inner = jnp.einsum("mkab,kjbq->mjaq", spectrum, inverse_inner, precision=highest)
    real_part = inner[:, 0]
    imag_part = inner[:, 1]
    twisted = jnp.stack(
        [
            real_part * cos_twist - imag_part * sin_twist,
            imag_part * cos_twist + real_part * sin_twist,
        ],
        axis=1,
    )
    signal = jnp.einsum("kna,mkab->nmb", outer_table, twisted, precision=highest)
    return signal / total_len


def spectral_work(pieces):
    gated_part, grad_part, filter_part = pieces
    half_rows = gated_part.shape[0]
    chan_total = gated_part.shape[1]
    item_count = filter_part.shape[1]
    group_size = chan_total // item_count
    seq_len = half_rows * radix_cols
    full_rows = 2 * half_rows
    total_len = 2 * seq_len
    cos_outer, sin_outer = phase_table(half_rows, full_rows, full_rows)
    cos_twist, sin_twist = phase_table(full_rows, radix_cols, total_len)
    cos_inner, sin_inner = phase_table(radix_cols, radix_cols, radix_cols)
    outer_table = jnp.stack([cos_outer, -sin_outer])
    forward_inner = jnp.stack(
        [jnp.stack([cos_inner, -sin_inner]), jnp.stack([sin_inner, cos_inner])]
    )
    inverse_inner = jnp.stack(
        [jnp.stack([cos_inner, sin_inner]), jnp.stack([-sin_inner, cos_inner])]
    )
    tables = (outer_table, cos_twist, sin_twist, forward_inner, inverse_inner)
    shaped = (item_count, group_size, 2, full_rows, radix_cols)
    flat_shape = (chan_total, 2, full_rows, radix_cols)
    signals = jnp.concatenate([gated_part, grad_part], axis=1).astype(wide_type)
    both_specs = forward_dft(signals, tables)
    gated_spec = both_specs[:chan_total].reshape(shaped)
    inner_spec = both_specs[chan_total:].reshape(shaped)
    filt_spec = forward_dft(filter_part.astype(wide_type), tables)[:, None]
    gated_re = gated_spec[:, :, 0]
    gated_im = gated_spec[:, :, 1]
    inner_re = inner_spec[:, :, 0]
    inner_im = inner_spec[:, :, 1]
    filt_re = filt_spec[:, :, 0]
    filt_im = filt_spec[:, :, 1]
    conv_spec = jnp.stack(
        [gated_re * filt_re - gated_im * filt_im, gated_re * filt_im + gated_im * filt_re], axis=2
    )
    back_spec = jnp.stack(
        [inner_re * filt_re + inner_im * filt_im, inner_im * filt_re - inner_re * filt_im], axis=2
    )
    corr_spec = jnp.stack(
        [inner_re * gated_re + inner_im * gated_im, inner_im * gated_re - inner_re * gated_im],
        axis=2,
    )
    signals_back = inverse_dft(
        jnp.concatenate([conv_spec.reshape(flat_shape), back_spec.reshape(flat_shape)], axis=0),
        tables,
        total_len,
    )
    scale = 1.0 / math.sqrt(seq_len * group_size)
    summed = jnp.sum(corr_spec, axis=1)
    lagged = (inverse_dft(summed, tables, total_len) * scale).astype(narrow_type)
    long_squares = jnp.sum(jnp.square(lagged.astype(wide_type)))
    stacked = jnp.concatenate([signals_back.astype(narrow_type), lagged], axis=1)
    return stacked, long_squares


def body(first_gate, second_gate, output_gate, values, cotangent, medium_filter, long_filter):
    tok_rows, chan_local = first_gate.shape
    tap_count, local_groups = medium_filter.shape
    group_size = chan_local // local_groups
    block_rows = math.gcd(tok_rows, block_limit)
    block_count = tok_rows // block_rows
    window_rows = block_rows + tap_count - 1
    ctx_devices = lax.axis_size("ctx")
    ctx_groups = local_groups // ctx_devices
    first_wide = first_gate.astype(wide_type)
    second_wide = second_gate.astype(wide_type)
    values_wide = values.astype(wide_type)
    cotangent_wide = cotangent.astype(wide_type)
    gated_input = (first_wide * values_wide).astype(narrow_type)
    prior_rim = passed_along(gated_input[tok_rows - tap_count + 1 :], "ctx", 1)
    extended = jnp.concatenate([prior_rim, gated_input], axis=0).reshape(
        tok_rows + tap_count - 1, local_groups, group_size
    )
    forward_win = windows_of(extended, block_rows, block_count, window_rows)
    mixed_first = jnp.einsum(
        "gij,bjgc->bigc",
        band_table(medium_filter, block_rows, True),
        forward_win,
        preferred_element_type=wide_type,
    ).reshape(tok_rows, chan_local)
    carried = (second_wide * mixed_first).astype(narrow_type)
    grad_inner = (cotangent_wide * output_gate.astype(wide_type)).astype(narrow_type)

    def token_major(matrix):
        return matrix.T.reshape(ctx_devices, -1, tok_rows)

    outbound = jnp.concatenate(
        [token_major(carried), token_major(grad_inner), token_major(long_filter)], axis=1
    )
    arrived = lax.all_to_all(outbound, "ctx", 0, 0, tiled=True)
    chan_share = ctx_groups * group_size
    returned, long_squares = spectral_work(
        (
            arrived[:, :chan_share],
            arrived[:, chan_share : 2 * chan_share],
            arrived[:, 2 * chan_share :],
        )
    )
    back = lax.all_to_all(returned, "ctx", 0, 0, tiled=True)
    second_mix = back[:, :chan_share].reshape(chan_local, tok_rows).T
    grad_carried = back[:, chan_share : 2 * chan_share].reshape(chan_local, tok_rows).T
    grad_carried = grad_carried.astype(wide_type)
    grad_long = back[:, 2 * chan_share :].reshape(local_groups, tok_rows).T
    grad_output_gate = (cotangent_wide * second_mix.astype(wide_type)).astype(narrow_type)
    grad_second = (grad_carried * mixed_first).astype(narrow_type)
    grad_mixed = (grad_carried * second_wide).astype(narrow_type)
    after_rim = passed_along(grad_mixed[: tap_count - 1], "ctx", -1)
    trailing = jnp.concatenate([grad_mixed, after_rim], axis=0).reshape(
        tok_rows + tap_count - 1, local_groups, group_size
    )
    backward_win = windows_of(trailing, block_rows, block_count, window_rows)
    grad_gated = jnp.einsum(
        "gij,bjgc->bigc",
        band_table(medium_filter, block_rows, False),
        backward_win,
        preferred_element_type=wide_type,
    ).reshape(tok_rows, chan_local)
    grad_first = (grad_gated * values_wide).astype(narrow_type)
    grad_values = (grad_gated * first_wide).astype(narrow_type)
    grad_blocks = grad_mixed.reshape(block_count, block_rows, local_groups, group_size)
    products = jnp.einsum(
        "bigc,bjgc->gij", grad_blocks, forward_win, preferred_element_type=wide_type
    )
    skewed = jnp.concatenate(
        [
            products.reshape(local_groups, block_rows * window_rows),
            jnp.zeros((local_groups, block_rows), wide_type),
        ],
        axis=1,
    )
    diagonal_sums = jnp.sum(
        skewed.reshape(local_groups, block_rows, window_rows + 1)[:, :, :tap_count], axis=1
    )
    scale = 1.0 / math.sqrt(tok_rows * ctx_devices * group_size)
    medium_terms = diagonal_sums[:, ::-1].T * scale
    tap_share = tap_count // ctx_devices
    pieces = lax.all_to_all(
        medium_terms.reshape(ctx_devices, tap_share, local_groups), "ctx", 0, 0, tiled=True
    )
    own_rows = jnp.sum(pieces, axis=0).reshape(1, tap_share * local_groups)
    own_squares = long_squares + jnp.sum(own_rows * own_rows)
    payload = jnp.concatenate([own_rows, own_squares.reshape(1, 1)], axis=1)
    gathered = lax.all_to_all(
        jnp.broadcast_to(payload, (ctx_devices, payload.shape[1])), "ctx", 0, 0, tiled=True
    )
    grad_medium = gathered[:, : tap_share * local_groups].reshape(tap_count, local_groups)
    ch_squares = jnp.sum(gathered[:, tap_share * local_groups])
    ch_devices = lax.axis_size("ch")
    ch_all = lax.all_to_all(
        jnp.broadcast_to(ch_squares.reshape(1, 1), (ch_devices, 1)), "ch", 0, 0, tiled=True
    )
    total_squares = jnp.sum(ch_all)
    entries = (tok_rows * ctx_devices + tap_count) * local_groups * ch_devices
    filter_rms = jnp.sqrt(total_squares / entries)
    return (
        grad_first,
        grad_second,
        grad_output_gate,
        grad_values,
        grad_medium,
        grad_long,
        filter_rms,
    )


def solution(mesh):
    return jax.shard_map(
        body,
        mesh=mesh,
        in_specs=(
            P("ctx", "ch"),
            P("ctx", "ch"),
            P("ctx", "ch"),
            P("ctx", "ch"),
            P("ctx", "ch"),
            P(None, "ch"),
            P("ctx", "ch"),
        ),
        out_specs=(
            P("ctx", "ch"),
            P("ctx", "ch"),
            P("ctx", "ch"),
            P("ctx", "ch"),
            P(None, "ch"),
            P("ctx", "ch"),
            P(),
        ),
        check_vma=False,
    )
```

```python
import math

import jax
import jax.numpy as jnp
from jax import lax
from jax.sharding import PartitionSpec as P

radix_cols = 128
block_limit = 64
highest = lax.Precision.HIGHEST
wide_type = jnp.float32
narrow_type = jnp.bfloat16


def passed_along(array, axis, by):
    peers = lax.axis_size(axis)
    pairs = [(i, i + by) for i in range(peers) if 0 <= i + by < peers]
    return lax.ppermute(array, axis, pairs)


def band_table(filt, block_rows, flipped):
    tap_count, group_count = filt.shape
    window_rows = block_rows + tap_count - 1
    leading = filt[::-1] if flipped else filt
    padded = jnp.concatenate([leading.T, jnp.zeros((group_count, block_rows), filt.dtype)], axis=1)
    tiled = jnp.broadcast_to(padded[:, None, :], (group_count, block_rows, window_rows + 1))
    tiled = tiled.reshape(group_count, block_rows * (window_rows + 1))
    return tiled[:, : block_rows * window_rows].reshape(group_count, block_rows, window_rows)


def windows_of(extended, block_rows, block_count, window_rows):
    return jnp.stack(
        [
            extended[number * block_rows : number * block_rows + window_rows]
            for number in range(block_count)
        ]
    )


def phase_table(row_count, col_count, period):
    row_ids = lax.broadcasted_iota(jnp.int32, (row_count, col_count), 0)
    col_ids = lax.broadcasted_iota(jnp.int32, (row_count, col_count), 1)
    angle = (row_ids * col_ids % period).astype(wide_type) * (2.0 * math.pi / period)
    return (jnp.cos(angle), jnp.sin(angle))


def forward_dft(signal, tables):
    outer_table, cos_twist, sin_twist, forward_inner, inverse_inner = tables
    outer = jnp.einsum("kna,nmb->mkab", outer_table, signal, precision=highest)
    real_part = outer[:, 0]
    imag_part = outer[:, 1]
    twisted = jnp.stack(
        [
            real_part * cos_twist + imag_part * sin_twist,
            imag_part * cos_twist - real_part * sin_twist,
        ],
        axis=1,
    )
    return jnp.einsum("mkab,kjbq->mjaq", twisted, forward_inner, precision=highest)


def inverse_dft(spectrum, tables, total_len):
    outer_table, cos_twist, sin_twist, forward_inner, inverse_inner = tables
    inner = jnp.einsum("mkab,kjbq->mjaq", spectrum, inverse_inner, precision=highest)
    real_part = inner[:, 0]
    imag_part = inner[:, 1]
    twisted = jnp.stack(
        [
            real_part * cos_twist - imag_part * sin_twist,
            imag_part * cos_twist + real_part * sin_twist,
        ],
        axis=1,
    )
    signal = jnp.einsum("kna,mkab->nmb", outer_table, twisted, precision=highest)
    return signal / total_len


def spectral_tables(half_rows):
    full_rows = 2 * half_rows
    total_len = 2 * half_rows * radix_cols
    cos_outer, sin_outer = phase_table(half_rows, full_rows, full_rows)
    cos_twist, sin_twist = phase_table(full_rows, radix_cols, total_len)
    cos_inner, sin_inner = phase_table(radix_cols, radix_cols, radix_cols)
    outer_table = jnp.stack([cos_outer, -sin_outer])
    forward_inner = jnp.stack(
        [jnp.stack([cos_inner, -sin_inner]), jnp.stack([sin_inner, cos_inner])]
    )
    inverse_inner = jnp.stack(
        [jnp.stack([cos_inner, sin_inner]), jnp.stack([-sin_inner, cos_inner])]
    )
    return (outer_table, cos_twist, sin_twist, forward_inner, inverse_inner)


def grouped_spec(part, tables, item_count):
    spec = forward_dft(part.astype(wide_type), tables)
    return spec.reshape((item_count, -1) + spec.shape[1:])


def spectral_back(grad_part, filter_part, tables):
    half_rows, chan_total = grad_part.shape[:2]
    item_count = filter_part.shape[1]
    total_len = 2 * half_rows * radix_cols
    inner_spec = grouped_spec(grad_part, tables, item_count)
    filt_spec = grouped_spec(filter_part, tables, item_count)
    inner_re = inner_spec[:, :, 0]
    inner_im = inner_spec[:, :, 1]
    filt_re = filt_spec[:, :, 0]
    filt_im = filt_spec[:, :, 1]
    back_spec = jnp.stack(
        [inner_re * filt_re + inner_im * filt_im, inner_im * filt_re - inner_re * filt_im], axis=2
    )
    flat_shape = (chan_total,) + back_spec.shape[2:]
    grad_carried = inverse_dft(back_spec.reshape(flat_shape), tables, total_len)
    return grad_carried.astype(narrow_type), inner_spec, filt_spec


def spectral_forward(gated_part, inner_spec, filt_spec, tables):
    half_rows, chan_total = gated_part.shape[:2]
    item_count = filt_spec.shape[0]
    group_size = chan_total // item_count
    seq_len = half_rows * radix_cols
    total_len = 2 * seq_len
    gated_spec = grouped_spec(gated_part, tables, item_count)
    gated_re = gated_spec[:, :, 0]
    gated_im = gated_spec[:, :, 1]
    inner_re = inner_spec[:, :, 0]
    inner_im = inner_spec[:, :, 1]
    filt_re = filt_spec[:, :, 0]
    filt_im = filt_spec[:, :, 1]
    conv_spec = jnp.stack(
        [gated_re * filt_re - gated_im * filt_im, gated_re * filt_im + gated_im * filt_re], axis=2
    )
    corr_spec = jnp.stack(
        [inner_re * gated_re + inner_im * gated_im, inner_im * gated_re - inner_re * gated_im],
        axis=2,
    )
    flat_shape = (chan_total,) + conv_spec.shape[2:]
    second_mix = inverse_dft(conv_spec.reshape(flat_shape), tables, total_len)
    scale = 1.0 / math.sqrt(seq_len * group_size)
    summed = jnp.sum(corr_spec, axis=1)
    lagged = (inverse_dft(summed, tables, total_len) * scale).astype(narrow_type)
    long_squares = jnp.sum(jnp.square(lagged.astype(wide_type)))
    stacked = jnp.concatenate([second_mix.astype(narrow_type), lagged], axis=1)
    return stacked, long_squares


def body(first_gate, second_gate, output_gate, values, cotangent, medium_filter, long_filter):
    tok_rows, chan_local = first_gate.shape
    tap_count, local_groups = medium_filter.shape
    group_size = chan_local // local_groups
    block_rows = math.gcd(tok_rows, block_limit)
    block_count = tok_rows // block_rows
    window_rows = block_rows + tap_count - 1
    ctx_devices = lax.axis_size("ctx")
    ctx_groups = local_groups // ctx_devices
    chan_share = ctx_groups * group_size

    def token_major(matrix):
        return matrix.T.reshape(ctx_devices, -1, tok_rows)

    cotangent_wide = cotangent.astype(wide_type)
    grad_inner = (cotangent_wide * output_gate.astype(wide_type)).astype(narrow_type)
    early_out = jnp.concatenate([token_major(grad_inner), token_major(long_filter)], axis=1)
    early_in = lax.all_to_all(early_out, "ctx", 0, 0, tiled=True)
    tables = spectral_tables(tok_rows // radix_cols * ctx_devices)
    carried_back, inner_spec, filt_spec = spectral_back(
        early_in[:, :chan_share], early_in[:, chan_share:], tables
    )
    carried_home = lax.all_to_all(carried_back, "ctx", 0, 0, tiled=True)
    grad_carried = carried_home.reshape(chan_local, tok_rows).T.astype(wide_type)

    first_wide = first_gate.astype(wide_type)
    second_wide = second_gate.astype(wide_type)
    values_wide = values.astype(wide_type)
    gated_input = (first_wide * values_wide).astype(narrow_type)
    prior_rim = passed_along(gated_input[tok_rows - tap_count + 1 :], "ctx", 1)
    extended = jnp.concatenate([prior_rim, gated_input], axis=0).reshape(
        tok_rows + tap_count - 1, local_groups, group_size
    )
    forward_win = windows_of(extended, block_rows, block_count, window_rows)
    mixed_first = jnp.einsum(
        "gij,bjgc->bigc",
        band_table(medium_filter, block_rows, True),
        forward_win,
        preferred_element_type=wide_type,
    ).reshape(tok_rows, chan_local)
    carried = (second_wide * mixed_first).astype(narrow_type)
    late_in = lax.all_to_all(token_major(carried), "ctx", 0, 0, tiled=True)
    returned, long_squares = spectral_forward(late_in, inner_spec, filt_spec, tables)
    back = lax.all_to_all(returned, "ctx", 0, 0, tiled=True)
    second_mix = back[:, :chan_share].reshape(chan_local, tok_rows).T
    grad_long = back[:, chan_share:].reshape(local_groups, tok_rows).T
    grad_output_gate = (cotangent_wide * second_mix.astype(wide_type)).astype(narrow_type)
    grad_second = (grad_carried * mixed_first).astype(narrow_type)
    grad_mixed = (grad_carried * second_wide).astype(narrow_type)
    after_rim = passed_along(grad_mixed[: tap_count - 1], "ctx", -1)
    trailing = jnp.concatenate([grad_mixed, after_rim], axis=0).reshape(
        tok_rows + tap_count - 1, local_groups, group_size
    )
    backward_win = windows_of(trailing, block_rows, block_count, window_rows)
    grad_gated = jnp.einsum(
        "gij,bjgc->bigc",
        band_table(medium_filter, block_rows, False),
        backward_win,
        preferred_element_type=wide_type,
    ).reshape(tok_rows, chan_local)
    grad_first = (grad_gated * values_wide).astype(narrow_type)
    grad_values = (grad_gated * first_wide).astype(narrow_type)
    grad_blocks = grad_mixed.reshape(block_count, block_rows, local_groups, group_size)
    products = jnp.einsum(
        "bigc,bjgc->gij", grad_blocks, forward_win, preferred_element_type=wide_type
    )
    skewed = jnp.concatenate(
        [
            products.reshape(local_groups, block_rows * window_rows),
            jnp.zeros((local_groups, block_rows), wide_type),
        ],
        axis=1,
    )
    diagonal_sums = jnp.sum(
        skewed.reshape(local_groups, block_rows, window_rows + 1)[:, :, :tap_count], axis=1
    )
    scale = 1.0 / math.sqrt(tok_rows * ctx_devices * group_size)
    medium_terms = diagonal_sums[:, ::-1].T * scale
    tap_share = tap_count // ctx_devices
    pieces = lax.all_to_all(
        medium_terms.reshape(ctx_devices, tap_share, local_groups), "ctx", 0, 0, tiled=True
    )
    own_rows = jnp.sum(pieces, axis=0).reshape(1, tap_share * local_groups)
    own_squares = long_squares + jnp.sum(own_rows * own_rows)
    payload = jnp.concatenate([own_rows, own_squares.reshape(1, 1)], axis=1)
    gathered = lax.all_to_all(
        jnp.broadcast_to(payload, (ctx_devices, payload.shape[1])), "ctx", 0, 0, tiled=True
    )
    grad_medium = gathered[:, : tap_share * local_groups].reshape(tap_count, local_groups)
    ch_squares = jnp.sum(gathered[:, tap_share * local_groups])
    ch_devices = lax.axis_size("ch")
    ch_all = lax.all_to_all(
        jnp.broadcast_to(ch_squares.reshape(1, 1), (ch_devices, 1)), "ch", 0, 0, tiled=True
    )
    total_squares = jnp.sum(ch_all)
    entries = (tok_rows * ctx_devices + tap_count) * local_groups * ch_devices
    filter_rms = jnp.sqrt(total_squares / entries)
    return (
        grad_first,
        grad_second,
        grad_output_gate,
        grad_values,
        grad_medium,
        grad_long,
        filter_rms,
    )


def solution(mesh):
    return jax.shard_map(
        body,
        mesh=mesh,
        in_specs=(
            P("ctx", "ch"),
            P("ctx", "ch"),
            P("ctx", "ch"),
            P("ctx", "ch"),
            P("ctx", "ch"),
            P(None, "ch"),
            P("ctx", "ch"),
        ),
        out_specs=(
            P("ctx", "ch"),
            P("ctx", "ch"),
            P("ctx", "ch"),
            P("ctx", "ch"),
            P(None, "ch"),
            P("ctx", "ch"),
            P(),
        ),
        check_vma=False,
    )
```

```python
import math

import jax
import jax.numpy as jnp
from jax import lax
from jax.sharding import PartitionSpec as P

radix_cols = 128
block_limit = 64
highest = lax.Precision.HIGHEST
wide_type = jnp.float32
narrow_type = jnp.bfloat16


def passed_along(array, axis, by):
    peers = lax.axis_size(axis)
    pairs = [(i, i + by) for i in range(peers) if 0 <= i + by < peers]
    return lax.ppermute(array, axis, pairs)


def band_table(filt, block_rows, flipped):
    tap_count, group_count = filt.shape
    window_rows = block_rows + tap_count - 1
    leading = filt[::-1] if flipped else filt
    padded = jnp.concatenate([leading.T, jnp.zeros((group_count, block_rows), filt.dtype)], axis=1)
    tiled = jnp.broadcast_to(padded[:, None, :], (group_count, block_rows, window_rows + 1))
    tiled = tiled.reshape(group_count, block_rows * (window_rows + 1))
    return tiled[:, : block_rows * window_rows].reshape(group_count, block_rows, window_rows)


def windows_of(extended, block_rows, block_count, window_rows):
    return jnp.stack(
        [
            extended[number * block_rows : number * block_rows + window_rows]
            for number in range(block_count)
        ]
    )


def phase_table(row_count, col_count, period):
    row_ids = lax.broadcasted_iota(jnp.int32, (row_count, col_count), 0)
    col_ids = lax.broadcasted_iota(jnp.int32, (row_count, col_count), 1)
    angle = (row_ids * col_ids % period).astype(wide_type) * (2.0 * math.pi / period)
    return (jnp.cos(angle), jnp.sin(angle))


def forward_dft(signal, tables):
    outer_table, cos_twist, sin_twist, forward_inner, inverse_inner = tables
    outer = jnp.einsum("kna,nmb->mkab", outer_table, signal, precision=highest)
    real_part = outer[:, 0]
    imag_part = outer[:, 1]
    twisted = jnp.stack(
        [
            real_part * cos_twist + imag_part * sin_twist,
            imag_part * cos_twist - real_part * sin_twist,
        ],
        axis=1,
    )
    return jnp.einsum("mkab,kjbq->mjaq", twisted, forward_inner, precision=highest)


def inverse_dft(spectrum, tables, total_len):
    outer_table, cos_twist, sin_twist, forward_inner, inverse_inner = tables
    inner = jnp.einsum("mkab,kjbq->mjaq", spectrum, inverse_inner, precision=highest)
    real_part = inner[:, 0]
    imag_part = inner[:, 1]
    twisted = jnp.stack(
        [
            real_part * cos_twist - imag_part * sin_twist,
            imag_part * cos_twist + real_part * sin_twist,
        ],
        axis=1,
    )
    signal = jnp.einsum("kna,mkab->nmb", outer_table, twisted, precision=highest)
    return signal / total_len


def split_wide(value):
    high = value.astype(narrow_type)
    low = (value - high.astype(wide_type)).astype(narrow_type)
    return high, low


def joined_wide(high, low):
    return high.astype(wide_type) + low.astype(wide_type)


def butterfly_sum(value, axis):
    peers = lax.axis_size(axis)
    step = 1
    while step < peers:
        pairs = [(i, i ^ step) for i in range(peers)]
        value = value + lax.ppermute(value, axis, pairs)
        step *= 2
    return value


def medium_bands(filt):
    tap_count, item_count = filt.shape
    bands = band_table(filt, tap_count, False)
    near = bands[:, :, :tap_count]
    far = jnp.concatenate(
        [bands[:, :, tap_count:], jnp.zeros((item_count, tap_count, 1), filt.dtype)], axis=2
    )
    return near, far


def channel_work(pieces, filt):
    gated_part, grad_part, gate_part, filter_part = pieces
    half_rows = gated_part.shape[0]
    chan_total = gated_part.shape[1]
    item_count = filter_part.shape[1]
    group_size = chan_total // item_count
    seq_len = half_rows * radix_cols
    full_rows = 2 * half_rows
    total_len = 2 * seq_len
    scale = 1.0 / math.sqrt(seq_len * group_size)
    by_item = (half_rows, item_count, group_size, radix_cols)
    near, far = medium_bands(filt)

    gated_items = gated_part.reshape(by_item)
    gated_prev = jnp.concatenate([jnp.zeros_like(gated_items[:1]), gated_items[:-1]], axis=0)
    mixed = (
        jnp.einsum("ngcs,gsr->ngcr", gated_items, near, preferred_element_type=wide_type)
        + jnp.einsum("ngcs,gsr->ngcr", gated_prev, far, preferred_element_type=wide_type)
    ).reshape(half_rows, chan_total, radix_cols)
    gate_wide = gate_part.astype(wide_type)
    carried = (gate_wide * mixed).astype(narrow_type)

    cos_outer, sin_outer = phase_table(half_rows, full_rows, full_rows)
    cos_twist, sin_twist = phase_table(full_rows, radix_cols, total_len)
    cos_inner, sin_inner = phase_table(radix_cols, radix_cols, radix_cols)
    outer_table = jnp.stack([cos_outer, -sin_outer])
    forward_inner = jnp.stack(
        [jnp.stack([cos_inner, -sin_inner]), jnp.stack([sin_inner, cos_inner])]
    )
    inverse_inner = jnp.stack(
        [jnp.stack([cos_inner, sin_inner]), jnp.stack([-sin_inner, cos_inner])]
    )
    tables = (outer_table, cos_twist, sin_twist, forward_inner, inverse_inner)
    shaped = (item_count, group_size, 2, full_rows, radix_cols)
    flat_shape = (chan_total, 2, full_rows, radix_cols)
    signals = jnp.concatenate([carried, grad_part], axis=1).astype(wide_type)
    both_specs = forward_dft(signals, tables)
    gated_spec = both_specs[:chan_total].reshape(shaped)
    inner_spec = both_specs[chan_total:].reshape(shaped)
    filt_spec = forward_dft(filter_part.astype(wide_type), tables)[:, None]
    gated_re = gated_spec[:, :, 0]
    gated_im = gated_spec[:, :, 1]
    inner_re = inner_spec[:, :, 0]
    inner_im = inner_spec[:, :, 1]
    filt_re = filt_spec[:, :, 0]
    filt_im = filt_spec[:, :, 1]
    conv_spec = jnp.stack(
        [gated_re * filt_re - gated_im * filt_im, gated_re * filt_im + gated_im * filt_re], axis=2
    )
    back_spec = jnp.stack(
        [inner_re * filt_re + inner_im * filt_im, inner_im * filt_re - inner_re * filt_im], axis=2
    )
    corr_spec = jnp.stack(
        [inner_re * gated_re + inner_im * gated_im, inner_im * gated_re - inner_re * gated_im],
        axis=2,
    )
    signals_back = inverse_dft(
        jnp.concatenate([conv_spec.reshape(flat_shape), back_spec.reshape(flat_shape)], axis=0),
        tables,
        total_len,
    )
    second_mix = signals_back[:, :chan_total].astype(narrow_type)
    grad_carried = signals_back[:, chan_total:].astype(narrow_type).astype(wide_type)
    summed = jnp.sum(corr_spec, axis=1)
    lagged = (inverse_dft(summed, tables, total_len) * scale).astype(narrow_type)

    grad_second = (grad_carried * mixed).astype(narrow_type)
    grad_mixed = (grad_carried * gate_wide).astype(narrow_type)
    mixed_items = grad_mixed.reshape(by_item)
    mixed_next = jnp.concatenate([mixed_items[1:], jnp.zeros_like(mixed_items[:1])], axis=0)
    grad_gated = (
        jnp.einsum("ngcs,grs->ngcr", mixed_items, near, preferred_element_type=wide_type)
        + jnp.einsum("ngcs,grs->ngcr", mixed_next, far, preferred_element_type=wide_type)
    ).reshape(half_rows, chan_total, radix_cols)
    tap_count = filt.shape[0]
    own_lags = jnp.einsum(
        "ngcs,ngcr->gsr", gated_items, mixed_items, preferred_element_type=wide_type
    )
    prev_lags = jnp.einsum(
        "ngcs,ngcr->gsr", gated_prev, mixed_items, preferred_element_type=wide_type
    )
    lag_table = jnp.concatenate([own_lags, prev_lags], axis=2).reshape(item_count, -1)
    lag_table = jnp.concatenate(
        [lag_table, jnp.zeros((item_count, tap_count), wide_type)], axis=1
    ).reshape(item_count, tap_count, 2 * tap_count + 1)
    grad_medium = jnp.sum(lag_table[:, :, :tap_count], axis=1) * scale
    squares = jnp.sum(jnp.square(lagged.astype(wide_type))) + jnp.sum(grad_medium * grad_medium)
    squares = butterfly_sum(squares, "ch")
    medium_high, medium_low = split_wide(grad_medium)
    squares_high, squares_low = split_wide(squares)
    squares_row = jnp.zeros((1, radix_cols), narrow_type)
    squares_row = squares_row.at[0, 0].set(squares_high).at[0, 1].set(squares_low)
    shared = jnp.concatenate([medium_high, medium_low, squares_row], axis=0)
    shared = jnp.broadcast_to(shared[None], (half_rows,) + shared.shape)
    return jnp.concatenate(
        [second_mix, grad_second, grad_gated.astype(narrow_type), lagged, shared], axis=1
    )


def body(first_gate, second_gate, output_gate, values, cotangent, medium_filter, long_filter):
    tok_rows, chan_local = first_gate.shape
    tap_count, local_groups = medium_filter.shape
    group_size = chan_local // local_groups
    ctx_devices = lax.axis_size("ctx")
    ctx_groups = local_groups // ctx_devices
    chan_share = ctx_groups * group_size
    first_wide = first_gate.astype(wide_type)
    values_wide = values.astype(wide_type)
    cotangent_wide = cotangent.astype(wide_type)
    gated_input = (first_wide * values_wide).astype(narrow_type)
    grad_inner = (cotangent_wide * output_gate.astype(wide_type)).astype(narrow_type)

    def token_major(matrix):
        return matrix.T.reshape(ctx_devices, -1, tok_rows)

    outbound = jnp.concatenate(
        [
            token_major(gated_input),
            token_major(grad_inner),
            token_major(second_gate),
            token_major(long_filter),
        ],
        axis=1,
    )
    arrived = lax.all_to_all(outbound, "ctx", 0, 0, tiled=True)
    own_filter = lax.dynamic_slice_in_dim(
        medium_filter, lax.axis_index("ctx") * ctx_groups, ctx_groups, axis=1
    )
    returned = channel_work(
        (
            arrived[:, :chan_share],
            arrived[:, chan_share : 2 * chan_share],
            arrived[:, 2 * chan_share : 3 * chan_share],
            arrived[:, 3 * chan_share :],
        ),
        own_filter,
    )
    back = lax.all_to_all(returned, "ctx", 0, 0, tiled=True)

    def token_rows(start, count):
        return back[:, start : start + count].reshape(ctx_devices * count, tok_rows).T

    second_mix = token_rows(0, chan_share)
    grad_second = token_rows(chan_share, chan_share)
    grad_gated = token_rows(2 * chan_share, chan_share).astype(wide_type)
    grad_long = token_rows(3 * chan_share, ctx_groups)
    grad_medium = joined_wide(
        token_rows(3 * chan_share + ctx_groups, ctx_groups),
        token_rows(3 * chan_share + 2 * ctx_groups, ctx_groups),
    )
    squares_row = back[:, 3 * chan_share + 3 * ctx_groups]
    total_squares = jnp.sum(joined_wide(squares_row[:, 0], squares_row[:, 1]))
    grad_output_gate = (cotangent_wide * second_mix.astype(wide_type)).astype(narrow_type)
    grad_first = (grad_gated * values_wide).astype(narrow_type)
    grad_values = (grad_gated * first_wide).astype(narrow_type)
    entries = (tok_rows * ctx_devices + tap_count) * local_groups * lax.axis_size("ch")
    filter_rms = jnp.sqrt(total_squares / entries)
    return (
        grad_first,
        grad_second,
        grad_output_gate,
        grad_values,
        grad_medium,
        grad_long,
        filter_rms,
    )


def solution(mesh):
    return jax.shard_map(
        body,
        mesh=mesh,
        in_specs=(
            P("ctx", "ch"),
            P("ctx", "ch"),
            P("ctx", "ch"),
            P("ctx", "ch"),
            P("ctx", "ch"),
            P(None, "ch"),
            P("ctx", "ch"),
        ),
        out_specs=(
            P("ctx", "ch"),
            P("ctx", "ch"),
            P("ctx", "ch"),
            P("ctx", "ch"),
            P(None, "ch"),
            P("ctx", "ch"),
            P(),
        ),
        check_vma=False,
    )
```

```python
import math

import jax
import jax.numpy as jnp
from jax import lax
from jax.sharding import PartitionSpec as P

radix_cols = 128
block_limit = 64
highest = lax.Precision.HIGHEST
wide_type = jnp.float32
narrow_type = jnp.bfloat16


def passed_along(array, axis, by):
    peers = lax.axis_size(axis)
    pairs = [(i, i + by) for i in range(peers) if 0 <= i + by < peers]
    return lax.ppermute(array, axis, pairs)


def band_table(filt, block_rows, flipped):
    tap_count, group_count = filt.shape
    window_rows = block_rows + tap_count - 1
    leading = filt[::-1] if flipped else filt
    padded = jnp.concatenate([leading.T, jnp.zeros((group_count, block_rows), filt.dtype)], axis=1)
    tiled = jnp.broadcast_to(padded[:, None, :], (group_count, block_rows, window_rows + 1))
    tiled = tiled.reshape(group_count, block_rows * (window_rows + 1))
    return tiled[:, : block_rows * window_rows].reshape(group_count, block_rows, window_rows)


def windows_of(extended, block_rows, block_count, window_rows):
    return jnp.stack(
        [
            extended[number * block_rows : number * block_rows + window_rows]
            for number in range(block_count)
        ]
    )


def phase_table(row_count, col_count, period):
    row_ids = lax.broadcasted_iota(jnp.int32, (row_count, col_count), 0)
    col_ids = lax.broadcasted_iota(jnp.int32, (row_count, col_count), 1)
    angle = (row_ids * col_ids % period).astype(wide_type) * (2.0 * math.pi / period)
    return (jnp.cos(angle), jnp.sin(angle))


def forward_dft(signal, tables):
    outer_table, cos_twist, sin_twist, forward_inner, inverse_inner = tables
    outer = jnp.einsum("kna,nmb->mkab", outer_table, signal, precision=highest)
    real_part = outer[:, 0]
    imag_part = outer[:, 1]
    twisted = jnp.stack(
        [
            real_part * cos_twist + imag_part * sin_twist,
            imag_part * cos_twist - real_part * sin_twist,
        ],
        axis=1,
    )
    return jnp.einsum("mkab,kjbq->mjaq", twisted, forward_inner, precision=highest)


def inverse_dft(spectrum, tables, total_len):
    outer_table, cos_twist, sin_twist, forward_inner, inverse_inner = tables
    inner = jnp.einsum("mkab,kjbq->mjaq", spectrum, inverse_inner, precision=highest)
    real_part = inner[:, 0]
    imag_part = inner[:, 1]
    twisted = jnp.stack(
        [
            real_part * cos_twist - imag_part * sin_twist,
            imag_part * cos_twist + real_part * sin_twist,
        ],
        axis=1,
    )
    signal = jnp.einsum("kna,mkab->nmb", outer_table, twisted, precision=highest)
    return signal / total_len


def split_wide(value):
    high = value.astype(narrow_type)
    low = (value - high.astype(wide_type)).astype(narrow_type)
    return high, low


def joined_wide(high, low):
    return high.astype(wide_type) + low.astype(wide_type)


def gathered_sum(value, axis):
    peers = lax.axis_size(axis)
    source = lax.axis_index(axis)
    slot_ids = lax.iota(jnp.int32, peers)
    slots = jnp.where(slot_ids == source, value, 0.0)
    for shift in range(1, peers):
        pairs = [(i, (i + shift) % peers) for i in range(peers)]
        got = lax.ppermute(value, axis, pairs)
        slots = slots + jnp.where(slot_ids == (source - shift) % peers, got, 0.0)
    return jnp.sum(slots)


def medium_bands(filt):
    tap_count, item_count = filt.shape
    bands = band_table(filt, tap_count, False)
    near = bands[:, :, :tap_count]
    far = jnp.concatenate(
        [bands[:, :, tap_count:], jnp.zeros((item_count, tap_count, 1), filt.dtype)], axis=2
    )
    return near, far


def channel_work(pieces, filt):
    gated_part, grad_part, gate_part, filter_part = pieces
    half_rows = gated_part.shape[0]
    chan_total = gated_part.shape[1]
    item_count = filter_part.shape[1]
    group_size = chan_total // item_count
    seq_len = half_rows * radix_cols
    full_rows = 2 * half_rows
    total_len = 2 * seq_len
    scale = 1.0 / math.sqrt(seq_len * group_size)
    by_item = (half_rows, item_count, group_size, radix_cols)
    near, far = medium_bands(filt)

    gated_items = gated_part.reshape(by_item)
    gated_prev = jnp.concatenate([jnp.zeros_like(gated_items[:1]), gated_items[:-1]], axis=0)
    mixed = (
        jnp.einsum("ngcs,gsr->ngcr", gated_items, near, preferred_element_type=wide_type)
        + jnp.einsum("ngcs,gsr->ngcr", gated_prev, far, preferred_element_type=wide_type)
    ).reshape(half_rows, chan_total, radix_cols)
    gate_wide = gate_part.astype(wide_type)
    carried = (gate_wide * mixed).astype(narrow_type)

    cos_outer, sin_outer = phase_table(half_rows, full_rows, full_rows)
    cos_twist, sin_twist = phase_table(full_rows, radix_cols, total_len)
    cos_inner, sin_inner = phase_table(radix_cols, radix_cols, radix_cols)
    outer_table = jnp.stack([cos_outer, -sin_outer])
    forward_inner = jnp.stack(
        [jnp.stack([cos_inner, -sin_inner]), jnp.stack([sin_inner, cos_inner])]
    )
    inverse_inner = jnp.stack(
        [jnp.stack([cos_inner, sin_inner]), jnp.stack([-sin_inner, cos_inner])]
    )
    tables = (outer_table, cos_twist, sin_twist, forward_inner, inverse_inner)
    shaped = (item_count, group_size, 2, full_rows, radix_cols)
    flat_shape = (chan_total, 2, full_rows, radix_cols)
    signals = jnp.concatenate([carried, grad_part], axis=1).astype(wide_type)
    both_specs = forward_dft(signals, tables)
    gated_spec = both_specs[:chan_total].reshape(shaped)
    inner_spec = both_specs[chan_total:].reshape(shaped)
    filt_spec = forward_dft(filter_part.astype(wide_type), tables)[:, None]
    gated_re = gated_spec[:, :, 0]
    gated_im = gated_spec[:, :, 1]
    inner_re = inner_spec[:, :, 0]
    inner_im = inner_spec[:, :, 1]
    filt_re = filt_spec[:, :, 0]
    filt_im = filt_spec[:, :, 1]
    conv_spec = jnp.stack(
        [gated_re * filt_re - gated_im * filt_im, gated_re * filt_im + gated_im * filt_re], axis=2
    )
    back_spec = jnp.stack(
        [inner_re * filt_re + inner_im * filt_im, inner_im * filt_re - inner_re * filt_im], axis=2
    )
    corr_spec = jnp.stack(
        [inner_re * gated_re + inner_im * gated_im, inner_im * gated_re - inner_re * gated_im],
        axis=2,
    )
    signals_back = inverse_dft(
        jnp.concatenate([conv_spec.reshape(flat_shape), back_spec.reshape(flat_shape)], axis=0),
        tables,
        total_len,
    )
    second_mix = signals_back[:, :chan_total].astype(narrow_type)
    grad_carried = signals_back[:, chan_total:].astype(narrow_type).astype(wide_type)
    summed = jnp.sum(corr_spec, axis=1)
    lagged = (inverse_dft(summed, tables, total_len) * scale).astype(narrow_type)

    grad_second = (grad_carried * mixed).astype(narrow_type)
    grad_mixed = (grad_carried * gate_wide).astype(narrow_type)
    mixed_items = grad_mixed.reshape(by_item)
    mixed_next = jnp.concatenate([mixed_items[1:], jnp.zeros_like(mixed_items[:1])], axis=0)
    grad_gated = (
        jnp.einsum("ngcs,grs->ngcr", mixed_items, near, preferred_element_type=wide_type)
        + jnp.einsum("ngcs,grs->ngcr", mixed_next, far, preferred_element_type=wide_type)
    ).reshape(half_rows, chan_total, radix_cols)
    tap_count = filt.shape[0]
    own_lags = jnp.einsum(
        "ngcs,ngcr->gsr", gated_items, mixed_items, preferred_element_type=wide_type
    )
    prev_lags = jnp.einsum(
        "ngcs,ngcr->gsr", gated_prev, mixed_items, preferred_element_type=wide_type
    )
    lag_table = jnp.concatenate([own_lags, prev_lags], axis=2).reshape(item_count, -1)
    lag_table = jnp.concatenate(
        [lag_table, jnp.zeros((item_count, tap_count), wide_type)], axis=1
    ).reshape(item_count, tap_count, 2 * tap_count + 1)
    grad_medium = jnp.sum(lag_table[:, :, :tap_count], axis=1) * scale
    squares = jnp.sum(jnp.square(lagged.astype(wide_type))) + jnp.sum(grad_medium * grad_medium)
    squares = gathered_sum(squares, "ch")
    medium_high, medium_low = split_wide(grad_medium)
    squares_high, squares_low = split_wide(squares)
    squares_row = jnp.concatenate(
        [
            squares_high.reshape(1, 1),
            squares_low.reshape(1, 1),
            jnp.zeros((1, radix_cols - 2), narrow_type),
        ],
        axis=1,
    )
    shared = jnp.concatenate([medium_high, medium_low, squares_row], axis=0)
    shared = jnp.broadcast_to(shared[None], (half_rows,) + shared.shape)
    return jnp.concatenate(
        [second_mix, grad_second, grad_gated.astype(narrow_type), lagged, shared], axis=1
    )


def body(first_gate, second_gate, output_gate, values, cotangent, medium_filter, long_filter):
    tok_rows, chan_local = first_gate.shape
    tap_count, local_groups = medium_filter.shape
    group_size = chan_local // local_groups
    ctx_devices = lax.axis_size("ctx")
    ctx_groups = local_groups // ctx_devices
    chan_share = ctx_groups * group_size
    first_wide = first_gate.astype(wide_type)
    values_wide = values.astype(wide_type)
    cotangent_wide = cotangent.astype(wide_type)
    gated_input = (first_wide * values_wide).astype(narrow_type)
    grad_inner = (cotangent_wide * output_gate.astype(wide_type)).astype(narrow_type)

    def token_major(matrix):
        return matrix.T.reshape(ctx_devices, -1, tok_rows)

    outbound = jnp.concatenate(
        [
            token_major(gated_input),
            token_major(grad_inner),
            token_major(second_gate),
            token_major(long_filter),
        ],
        axis=1,
    )
    arrived = lax.all_to_all(outbound, "ctx", 0, 0, tiled=True)
    own_filter = lax.dynamic_slice_in_dim(
        medium_filter, lax.axis_index("ctx") * ctx_groups, ctx_groups, axis=1
    )
    returned = channel_work(
        (
            arrived[:, :chan_share],
            arrived[:, chan_share : 2 * chan_share],
            arrived[:, 2 * chan_share : 3 * chan_share],
            arrived[:, 3 * chan_share :],
        ),
        own_filter,
    )
    back = lax.all_to_all(returned, "ctx", 0, 0, tiled=True)

    def token_rows(start, count):
        return back[:, start : start + count].reshape(ctx_devices * count, tok_rows).T

    second_mix = token_rows(0, chan_share)
    grad_second = token_rows(chan_share, chan_share)
    grad_gated = token_rows(2 * chan_share, chan_share).astype(wide_type)
    grad_long = token_rows(3 * chan_share, ctx_groups)
    grad_medium = joined_wide(
        token_rows(3 * chan_share + ctx_groups, ctx_groups),
        token_rows(3 * chan_share + 2 * ctx_groups, ctx_groups),
    )
    squares_row = back[:, 3 * chan_share + 3 * ctx_groups]
    total_squares = jnp.sum(joined_wide(squares_row[:, 0], squares_row[:, 1]))
    grad_output_gate = (cotangent_wide * second_mix.astype(wide_type)).astype(narrow_type)
    grad_first = (grad_gated * values_wide).astype(narrow_type)
    grad_values = (grad_gated * first_wide).astype(narrow_type)
    entries = (tok_rows * ctx_devices + tap_count) * local_groups * lax.axis_size("ch")
    filter_rms = jnp.sqrt(total_squares / entries)
    return (
        grad_first,
        grad_second,
        grad_output_gate,
        grad_values,
        grad_medium,
        grad_long,
        filter_rms,
    )


def solution(mesh):
    return jax.shard_map(
        body,
        mesh=mesh,
        in_specs=(
            P("ctx", "ch"),
            P("ctx", "ch"),
            P("ctx", "ch"),
            P("ctx", "ch"),
            P("ctx", "ch"),
            P(None, "ch"),
            P("ctx", "ch"),
        ),
        out_specs=(
            P("ctx", "ch"),
            P("ctx", "ch"),
            P("ctx", "ch"),
            P("ctx", "ch"),
            P(None, "ch"),
            P("ctx", "ch"),
            P(),
        ),
        check_vma=False,
    )
```

```python
import math

import jax
import jax.numpy as jnp
from jax import lax
from jax.sharding import PartitionSpec as P

radix_cols = 128
block_limit = 64
highest = lax.Precision.HIGH
wide_type = jnp.float32
narrow_type = jnp.bfloat16


def passed_along(array, axis, by):
    peers = lax.axis_size(axis)
    pairs = [(i, i + by) for i in range(peers) if 0 <= i + by < peers]
    return lax.ppermute(array, axis, pairs)


def band_table(filt, block_rows, flipped):
    tap_count, group_count = filt.shape
    window_rows = block_rows + tap_count - 1
    leading = filt[::-1] if flipped else filt
    padded = jnp.concatenate([leading.T, jnp.zeros((group_count, block_rows), filt.dtype)], axis=1)
    tiled = jnp.broadcast_to(padded[:, None, :], (group_count, block_rows, window_rows + 1))
    tiled = tiled.reshape(group_count, block_rows * (window_rows + 1))
    return tiled[:, : block_rows * window_rows].reshape(group_count, block_rows, window_rows)


def windows_of(extended, block_rows, block_count, window_rows):
    return jnp.stack(
        [
            extended[number * block_rows : number * block_rows + window_rows]
            for number in range(block_count)
        ]
    )


def phase_table(row_count, col_count, period):
    row_ids = lax.broadcasted_iota(jnp.int32, (row_count, col_count), 0)
    col_ids = lax.broadcasted_iota(jnp.int32, (row_count, col_count), 1)
    angle = (row_ids * col_ids % period).astype(wide_type) * (2.0 * math.pi / period)
    return (jnp.cos(angle), jnp.sin(angle))


def forward_dft(signal, tables):
    outer_table, cos_twist, sin_twist, forward_inner, inverse_inner = tables
    outer = jnp.einsum("kna,nmb->mkab", outer_table, signal, precision=highest)
    real_part = outer[:, 0]
    imag_part = outer[:, 1]
    twisted = jnp.stack(
        [
            real_part * cos_twist + imag_part * sin_twist,
            imag_part * cos_twist - real_part * sin_twist,
        ],
        axis=1,
    )
    return jnp.einsum("mkab,kjbq->mjaq", twisted, forward_inner, precision=highest)


def inverse_dft(spectrum, tables, total_len):
    outer_table, cos_twist, sin_twist, forward_inner, inverse_inner = tables
    inner = jnp.einsum("mkab,kjbq->mjaq", spectrum, inverse_inner, precision=highest)
    real_part = inner[:, 0]
    imag_part = inner[:, 1]
    twisted = jnp.stack(
        [
            real_part * cos_twist - imag_part * sin_twist,
            imag_part * cos_twist + real_part * sin_twist,
        ],
        axis=1,
    )
    signal = jnp.einsum("kna,mkab->nmb", outer_table, twisted, precision=highest)
    return signal / total_len


def split_wide(value):
    high = value.astype(narrow_type)
    low = (value - high.astype(wide_type)).astype(narrow_type)
    return high, low


def joined_wide(high, low):
    return high.astype(wide_type) + low.astype(wide_type)


def butterfly_sum(value, axis):
    peers = lax.axis_size(axis)
    step = 1
    while step < peers:
        pairs = [(i, i ^ step) for i in range(peers)]
        value = value + lax.ppermute(value, axis, pairs)
        step *= 2
    return value


def medium_bands(filt):
    tap_count, item_count = filt.shape
    bands = band_table(filt, tap_count, False)
    near = bands[:, :, :tap_count]
    far = jnp.concatenate(
        [bands[:, :, tap_count:], jnp.zeros((item_count, tap_count, 1), filt.dtype)], axis=2
    )
    return near, far


def channel_work(pieces, filt):
    gated_part, grad_part, gate_part, filter_part = pieces
    half_rows = gated_part.shape[0]
    chan_total = gated_part.shape[1]
    item_count = filter_part.shape[1]
    group_size = chan_total // item_count
    seq_len = half_rows * radix_cols
    full_rows = 2 * half_rows
    total_len = 2 * seq_len
    scale = 1.0 / math.sqrt(seq_len * group_size)
    by_item = (half_rows, item_count, group_size, radix_cols)
    near, far = medium_bands(filt)

    gated_items = gated_part.reshape(by_item)
    gated_prev = jnp.concatenate([jnp.zeros_like(gated_items[:1]), gated_items[:-1]], axis=0)
    mixed = (
        jnp.einsum("ngcs,gsr->ngcr", gated_items, near, preferred_element_type=wide_type)
        + jnp.einsum("ngcs,gsr->ngcr", gated_prev, far, preferred_element_type=wide_type)
    ).reshape(half_rows, chan_total, radix_cols)
    gate_wide = gate_part.astype(wide_type)
    carried = (gate_wide * mixed).astype(narrow_type)

    cos_outer, sin_outer = phase_table(half_rows, full_rows, full_rows)
    cos_twist, sin_twist = phase_table(full_rows, radix_cols, total_len)
    cos_inner, sin_inner = phase_table(radix_cols, radix_cols, radix_cols)
    outer_table = jnp.stack([cos_outer, -sin_outer])
    forward_inner = jnp.stack(
        [jnp.stack([cos_inner, -sin_inner]), jnp.stack([sin_inner, cos_inner])]
    )
    inverse_inner = jnp.stack(
        [jnp.stack([cos_inner, sin_inner]), jnp.stack([-sin_inner, cos_inner])]
    )
    tables = (outer_table, cos_twist, sin_twist, forward_inner, inverse_inner)
    shaped = (item_count, group_size, 2, full_rows, radix_cols)
    flat_shape = (chan_total, 2, full_rows, radix_cols)
    signals = jnp.concatenate([carried, grad_part], axis=1).astype(wide_type)
    both_specs = forward_dft(signals, tables)
    gated_spec = both_specs[:chan_total].reshape(shaped)
    inner_spec = both_specs[chan_total:].reshape(shaped)
    filt_spec = forward_dft(filter_part.astype(wide_type), tables)[:, None]
    gated_re = gated_spec[:, :, 0]
    gated_im = gated_spec[:, :, 1]
    inner_re = inner_spec[:, :, 0]
    inner_im = inner_spec[:, :, 1]
    filt_re = filt_spec[:, :, 0]
    filt_im = filt_spec[:, :, 1]
    conv_spec = jnp.stack(
        [gated_re * filt_re - gated_im * filt_im, gated_re * filt_im + gated_im * filt_re], axis=2
    )
    back_spec = jnp.stack(
        [inner_re * filt_re + inner_im * filt_im, inner_im * filt_re - inner_re * filt_im], axis=2
    )
    corr_spec = jnp.stack(
        [inner_re * gated_re + inner_im * gated_im, inner_im * gated_re - inner_re * gated_im],
        axis=2,
    )
    signals_back = inverse_dft(
        jnp.concatenate([conv_spec.reshape(flat_shape), back_spec.reshape(flat_shape)], axis=0),
        tables,
        total_len,
    )
    second_mix = signals_back[:, :chan_total].astype(narrow_type)
    grad_carried = signals_back[:, chan_total:].astype(narrow_type).astype(wide_type)
    summed = jnp.sum(corr_spec, axis=1)
    lagged = (inverse_dft(summed, tables, total_len) * scale).astype(narrow_type)

    grad_second = (grad_carried * mixed).astype(narrow_type)
    grad_mixed = (grad_carried * gate_wide).astype(narrow_type)
    mixed_items = grad_mixed.reshape(by_item)
    mixed_next = jnp.concatenate([mixed_items[1:], jnp.zeros_like(mixed_items[:1])], axis=0)
    grad_gated = (
        jnp.einsum("ngcs,grs->ngcr", mixed_items, near, preferred_element_type=wide_type)
        + jnp.einsum("ngcs,grs->ngcr", mixed_next, far, preferred_element_type=wide_type)
    ).reshape(half_rows, chan_total, radix_cols)
    tap_count = filt.shape[0]
    own_lags = jnp.einsum(
        "ngcs,ngcr->gsr", gated_items, mixed_items, preferred_element_type=wide_type
    )
    prev_lags = jnp.einsum(
        "ngcs,ngcr->gsr", gated_prev, mixed_items, preferred_element_type=wide_type
    )
    lag_table = jnp.concatenate([own_lags, prev_lags], axis=2).reshape(item_count, -1)
    lag_table = jnp.concatenate(
        [lag_table, jnp.zeros((item_count, tap_count), wide_type)], axis=1
    ).reshape(item_count, tap_count, 2 * tap_count + 1)
    grad_medium = jnp.sum(lag_table[:, :, :tap_count], axis=1) * scale
    squares = jnp.sum(jnp.square(lagged.astype(wide_type))) + jnp.sum(grad_medium * grad_medium)
    squares = butterfly_sum(squares, "ch")
    medium_high, medium_low = split_wide(grad_medium)
    squares_high, squares_low = split_wide(squares)
    squares_row = jnp.zeros((1, radix_cols), narrow_type)
    squares_row = squares_row.at[0, 0].set(squares_high).at[0, 1].set(squares_low)
    shared = jnp.concatenate([medium_high, medium_low, squares_row], axis=0)
    shared = jnp.broadcast_to(shared[None], (half_rows,) + shared.shape)
    return jnp.concatenate(
        [second_mix, grad_second, grad_gated.astype(narrow_type), lagged, shared], axis=1
    )


def body(first_gate, second_gate, output_gate, values, cotangent, medium_filter, long_filter):
    tok_rows, chan_local = first_gate.shape
    tap_count, local_groups = medium_filter.shape
    group_size = chan_local // local_groups
    ctx_devices = lax.axis_size("ctx")
    ctx_groups = local_groups // ctx_devices
    chan_share = ctx_groups * group_size
    first_wide = first_gate.astype(wide_type)
    values_wide = values.astype(wide_type)
    cotangent_wide = cotangent.astype(wide_type)
    gated_input = (first_wide * values_wide).astype(narrow_type)
    grad_inner = (cotangent_wide * output_gate.astype(wide_type)).astype(narrow_type)

    def token_major(matrix):
        return matrix.T.reshape(ctx_devices, -1, tok_rows)

    outbound = jnp.concatenate(
        [
            token_major(gated_input),
            token_major(grad_inner),
            token_major(second_gate),
            token_major(long_filter),
        ],
        axis=1,
    )
    arrived = lax.all_to_all(outbound, "ctx", 0, 0, tiled=True)
    own_filter = lax.dynamic_slice_in_dim(
        medium_filter, lax.axis_index("ctx") * ctx_groups, ctx_groups, axis=1
    )
    returned = channel_work(
        (
            arrived[:, :chan_share],
            arrived[:, chan_share : 2 * chan_share],
            arrived[:, 2 * chan_share : 3 * chan_share],
            arrived[:, 3 * chan_share :],
        ),
        own_filter,
    )
    back = lax.all_to_all(returned, "ctx", 0, 0, tiled=True)

    def token_rows(start, count):
        return back[:, start : start + count].reshape(ctx_devices * count, tok_rows).T

    second_mix = token_rows(0, chan_share)
    grad_second = token_rows(chan_share, chan_share)
    grad_gated = token_rows(2 * chan_share, chan_share).astype(wide_type)
    grad_long = token_rows(3 * chan_share, ctx_groups)
    grad_medium = joined_wide(
        token_rows(3 * chan_share + ctx_groups, ctx_groups),
        token_rows(3 * chan_share + 2 * ctx_groups, ctx_groups),
    )
    squares_row = back[:, 3 * chan_share + 3 * ctx_groups]
    total_squares = jnp.sum(joined_wide(squares_row[:, 0], squares_row[:, 1]))
    grad_output_gate = (cotangent_wide * second_mix.astype(wide_type)).astype(narrow_type)
    grad_first = (grad_gated * values_wide).astype(narrow_type)
    grad_values = (grad_gated * first_wide).astype(narrow_type)
    entries = (tok_rows * ctx_devices + tap_count) * local_groups * lax.axis_size("ch")
    filter_rms = jnp.sqrt(total_squares / entries)
    return (
        grad_first,
        grad_second,
        grad_output_gate,
        grad_values,
        grad_medium,
        grad_long,
        filter_rms,
    )


def solution(mesh):
    return jax.shard_map(
        body,
        mesh=mesh,
        in_specs=(
            P("ctx", "ch"),
            P("ctx", "ch"),
            P("ctx", "ch"),
            P("ctx", "ch"),
            P("ctx", "ch"),
            P(None, "ch"),
            P("ctx", "ch"),
        ),
        out_specs=(
            P("ctx", "ch"),
            P("ctx", "ch"),
            P("ctx", "ch"),
            P("ctx", "ch"),
            P(None, "ch"),
            P("ctx", "ch"),
            P(),
        ),
        check_vma=False,
    )
```

```python
import math

import jax
import jax.numpy as jnp
from jax import lax
from jax.sharding import PartitionSpec as P

radix_cols = 128
block_limit = 64
highest = lax.Precision.HIGH
wide_type = jnp.float32
narrow_type = jnp.bfloat16


def passed_along(array, axis, by):
    peers = lax.axis_size(axis)
    pairs = [(i, i + by) for i in range(peers) if 0 <= i + by < peers]
    return lax.ppermute(array, axis, pairs)


def band_table(filt, block_rows, flipped):
    tap_count, group_count = filt.shape
    window_rows = block_rows + tap_count - 1
    leading = filt[::-1] if flipped else filt
    padded = jnp.concatenate([leading.T, jnp.zeros((group_count, block_rows), filt.dtype)], axis=1)
    tiled = jnp.broadcast_to(padded[:, None, :], (group_count, block_rows, window_rows + 1))
    tiled = tiled.reshape(group_count, block_rows * (window_rows + 1))
    return tiled[:, : block_rows * window_rows].reshape(group_count, block_rows, window_rows)


def windows_of(extended, block_rows, block_count, window_rows):
    return jnp.stack(
        [
            extended[number * block_rows : number * block_rows + window_rows]
            for number in range(block_count)
        ]
    )


def phase_table(row_count, col_count, period):
    row_ids = lax.broadcasted_iota(jnp.int32, (row_count, col_count), 0)
    col_ids = lax.broadcasted_iota(jnp.int32, (row_count, col_count), 1)
    angle = (row_ids * col_ids % period).astype(wide_type) * (2.0 * math.pi / period)
    return (jnp.cos(angle), jnp.sin(angle))


def forward_dft(signal, tables):
    outer_table, cos_twist, sin_twist, forward_inner, inverse_inner = tables
    outer = jnp.einsum("kna,nmb->mkab", outer_table, signal, precision=highest)
    real_part = outer[:, 0]
    imag_part = outer[:, 1]
    twisted = jnp.stack(
        [
            real_part * cos_twist + imag_part * sin_twist,
            imag_part * cos_twist - real_part * sin_twist,
        ],
        axis=1,
    )
    return jnp.einsum("mkab,kjbq->mjaq", twisted, forward_inner, precision=highest)


def inverse_dft(spectrum, tables, total_len):
    outer_table, cos_twist, sin_twist, forward_inner, inverse_inner = tables
    inner = jnp.einsum("mkab,kjbq->mjaq", spectrum, inverse_inner, precision=highest)
    real_part = inner[:, 0]
    imag_part = inner[:, 1]
    twisted = jnp.stack(
        [
            real_part * cos_twist - imag_part * sin_twist,
            imag_part * cos_twist + real_part * sin_twist,
        ],
        axis=1,
    )
    signal = jnp.einsum("kna,mkab->nmb", outer_table, twisted, precision=highest)
    return signal / total_len


def split_wide(value):
    high = value.astype(narrow_type)
    low = (value - high.astype(wide_type)).astype(narrow_type)
    return high, low


def joined_wide(high, low):
    return high.astype(wide_type) + low.astype(wide_type)


def medium_bands(filt):
    tap_count, item_count = filt.shape
    bands = band_table(filt, tap_count, False)
    near = bands[:, :, :tap_count]
    far = jnp.concatenate(
        [bands[:, :, tap_count:], jnp.zeros((item_count, tap_count, 1), filt.dtype)], axis=2
    )
    return near, far


def channel_work(pieces, filt):
    gated_part, grad_part, gate_part, filter_part = pieces
    half_rows = gated_part.shape[0]
    chan_total = gated_part.shape[1]
    item_count = filter_part.shape[1]
    group_size = chan_total // item_count
    seq_len = half_rows * radix_cols
    full_rows = 2 * half_rows
    total_len = 2 * seq_len
    scale = 1.0 / math.sqrt(seq_len * group_size)
    by_item = (half_rows, item_count, group_size, radix_cols)
    near, far = medium_bands(filt)

    gated_items = gated_part.reshape(by_item)
    gated_prev = jnp.concatenate([jnp.zeros_like(gated_items[:1]), gated_items[:-1]], axis=0)
    mixed = (
        jnp.einsum("ngcs,gsr->ngcr", gated_items, near, preferred_element_type=wide_type)
        + jnp.einsum("ngcs,gsr->ngcr", gated_prev, far, preferred_element_type=wide_type)
    ).reshape(half_rows, chan_total, radix_cols)
    gate_wide = gate_part.astype(wide_type)
    carried = (gate_wide * mixed).astype(narrow_type)

    cos_outer, sin_outer = phase_table(half_rows, full_rows, full_rows)
    cos_twist, sin_twist = phase_table(full_rows, radix_cols, total_len)
    cos_inner, sin_inner = phase_table(radix_cols, radix_cols, radix_cols)
    outer_table = jnp.stack([cos_outer, -sin_outer])
    forward_inner = jnp.stack(
        [jnp.stack([cos_inner, -sin_inner]), jnp.stack([sin_inner, cos_inner])]
    )
    inverse_inner = jnp.stack(
        [jnp.stack([cos_inner, sin_inner]), jnp.stack([-sin_inner, cos_inner])]
    )
    tables = (outer_table, cos_twist, sin_twist, forward_inner, inverse_inner)
    shaped = (item_count, group_size, 2, full_rows, radix_cols)
    flat_shape = (chan_total, 2, full_rows, radix_cols)
    signals = jnp.concatenate([carried, grad_part], axis=1).astype(wide_type)
    both_specs = forward_dft(signals, tables)
    gated_spec = both_specs[:chan_total].reshape(shaped)
    inner_spec = both_specs[chan_total:].reshape(shaped)
    filt_spec = forward_dft(filter_part.astype(wide_type), tables)[:, None]
    gated_re = gated_spec[:, :, 0]
    gated_im = gated_spec[:, :, 1]
    inner_re = inner_spec[:, :, 0]
    inner_im = inner_spec[:, :, 1]
    filt_re = filt_spec[:, :, 0]
    filt_im = filt_spec[:, :, 1]
    conv_spec = jnp.stack(
        [gated_re * filt_re - gated_im * filt_im, gated_re * filt_im + gated_im * filt_re], axis=2
    )
    back_spec = jnp.stack(
        [inner_re * filt_re + inner_im * filt_im, inner_im * filt_re - inner_re * filt_im], axis=2
    )
    corr_spec = jnp.stack(
        [inner_re * gated_re + inner_im * gated_im, inner_im * gated_re - inner_re * gated_im],
        axis=2,
    )
    signals_back = inverse_dft(
        jnp.concatenate([conv_spec.reshape(flat_shape), back_spec.reshape(flat_shape)], axis=0),
        tables,
        total_len,
    )
    second_mix = signals_back[:, :chan_total].astype(narrow_type)
    grad_carried = signals_back[:, chan_total:].astype(narrow_type).astype(wide_type)
    summed = jnp.sum(corr_spec, axis=1)
    lagged = (inverse_dft(summed, tables, total_len) * scale).astype(narrow_type)

    grad_second = (grad_carried * mixed).astype(narrow_type)
    grad_mixed = (grad_carried * gate_wide).astype(narrow_type)
    mixed_items = grad_mixed.reshape(by_item)
    mixed_next = jnp.concatenate([mixed_items[1:], jnp.zeros_like(mixed_items[:1])], axis=0)
    grad_gated = (
        jnp.einsum("ngcs,grs->ngcr", mixed_items, near, preferred_element_type=wide_type)
        + jnp.einsum("ngcs,grs->ngcr", mixed_next, far, preferred_element_type=wide_type)
    ).reshape(half_rows, chan_total, radix_cols)
    tap_count = filt.shape[0]
    own_lags = jnp.einsum(
        "ngcs,ngcr->gsr", gated_items, mixed_items, preferred_element_type=wide_type
    )
    prev_lags = jnp.einsum(
        "ngcs,ngcr->gsr", gated_prev, mixed_items, preferred_element_type=wide_type
    )
    lag_table = jnp.concatenate([own_lags, prev_lags], axis=2).reshape(item_count, -1)
    lag_table = jnp.concatenate(
        [lag_table, jnp.zeros((item_count, tap_count), wide_type)], axis=1
    ).reshape(item_count, tap_count, 2 * tap_count + 1)
    grad_medium = jnp.sum(lag_table[:, :, :tap_count], axis=1) * scale
    squares = jnp.sum(jnp.square(lagged.astype(wide_type))) + jnp.sum(grad_medium * grad_medium)
    squares = lax.psum(squares, "ch")
    medium_high, medium_low = split_wide(grad_medium)
    squares_high, squares_low = split_wide(squares)
    squares_row = jnp.concatenate(
        [
            squares_high.reshape(1, 1),
            squares_low.reshape(1, 1),
            jnp.zeros((1, radix_cols - 2), narrow_type),
        ],
        axis=1,
    )
    shared = jnp.concatenate([medium_high, medium_low, squares_row], axis=0)
    shared = jnp.broadcast_to(shared[None], (half_rows,) + shared.shape)
    return jnp.concatenate(
        [second_mix, grad_second, grad_gated.astype(narrow_type), lagged, shared], axis=1
    )


def body(first_gate, second_gate, output_gate, values, cotangent, medium_filter, long_filter):
    tok_rows, chan_local = first_gate.shape
    tap_count, local_groups = medium_filter.shape
    group_size = chan_local // local_groups
    ctx_devices = lax.axis_size("ctx")
    ctx_groups = local_groups // ctx_devices
    chan_share = ctx_groups * group_size
    first_wide = first_gate.astype(wide_type)
    values_wide = values.astype(wide_type)
    cotangent_wide = cotangent.astype(wide_type)
    gated_input = (first_wide * values_wide).astype(narrow_type)
    grad_inner = (cotangent_wide * output_gate.astype(wide_type)).astype(narrow_type)

    def token_major(matrix):
        return matrix.T.reshape(ctx_devices, -1, tok_rows)

    outbound = jnp.concatenate(
        [
            token_major(gated_input),
            token_major(grad_inner),
            token_major(second_gate),
            token_major(long_filter),
        ],
        axis=1,
    )
    arrived = lax.all_to_all(outbound, "ctx", 0, 0, tiled=True)
    own_filter = lax.dynamic_slice_in_dim(
        medium_filter, lax.axis_index("ctx") * ctx_groups, ctx_groups, axis=1
    )
    returned = channel_work(
        (
            arrived[:, :chan_share],
            arrived[:, chan_share : 2 * chan_share],
            arrived[:, 2 * chan_share : 3 * chan_share],
            arrived[:, 3 * chan_share :],
        ),
        own_filter,
    )
    back = lax.all_to_all(returned, "ctx", 0, 0, tiled=True)

    def token_rows(start, count):
        return back[:, start : start + count].reshape(ctx_devices * count, tok_rows).T

    second_mix = token_rows(0, chan_share)
    grad_second = token_rows(chan_share, chan_share)
    grad_gated = token_rows(2 * chan_share, chan_share).astype(wide_type)
    grad_long = token_rows(3 * chan_share, ctx_groups)
    grad_medium = joined_wide(
        token_rows(3 * chan_share + ctx_groups, ctx_groups),
        token_rows(3 * chan_share + 2 * ctx_groups, ctx_groups),
    )
    squares_row = back[:, 3 * chan_share + 3 * ctx_groups]
    total_squares = jnp.sum(joined_wide(squares_row[:, 0], squares_row[:, 1]))
    grad_output_gate = (cotangent_wide * second_mix.astype(wide_type)).astype(narrow_type)
    grad_first = (grad_gated * values_wide).astype(narrow_type)
    grad_values = (grad_gated * first_wide).astype(narrow_type)
    entries = (tok_rows * ctx_devices + tap_count) * local_groups * lax.axis_size("ch")
    filter_rms = jnp.sqrt(total_squares / entries)
    return (
        grad_first,
        grad_second,
        grad_output_gate,
        grad_values,
        grad_medium,
        grad_long,
        filter_rms,
    )


def solution(mesh):
    return jax.shard_map(
        body,
        mesh=mesh,
        in_specs=(
            P("ctx", "ch"),
            P("ctx", "ch"),
            P("ctx", "ch"),
            P("ctx", "ch"),
            P("ctx", "ch"),
            P(None, "ch"),
            P("ctx", "ch"),
        ),
        out_specs=(
            P("ctx", "ch"),
            P("ctx", "ch"),
            P("ctx", "ch"),
            P("ctx", "ch"),
            P(None, "ch"),
            P("ctx", "ch"),
            P(),
        ),
        check_vma=False,
    )
```

```python
import math

import jax
import jax.numpy as jnp
from jax import lax
from jax.sharding import PartitionSpec as P

radix_cols = 128
block_limit = 64
highest = lax.Precision.HIGH
wide_type = jnp.float32
narrow_type = jnp.bfloat16


def passed_along(array, axis, by):
    peers = lax.axis_size(axis)
    pairs = [(i, i + by) for i in range(peers) if 0 <= i + by < peers]
    return lax.ppermute(array, axis, pairs)


def band_table(filt, block_rows, flipped):
    tap_count, group_count = filt.shape
    window_rows = block_rows + tap_count - 1
    leading = filt[::-1] if flipped else filt
    padded = jnp.concatenate([leading.T, jnp.zeros((group_count, block_rows), filt.dtype)], axis=1)
    tiled = jnp.broadcast_to(padded[:, None, :], (group_count, block_rows, window_rows + 1))
    tiled = tiled.reshape(group_count, block_rows * (window_rows + 1))
    return tiled[:, : block_rows * window_rows].reshape(group_count, block_rows, window_rows)


def windows_of(extended, block_rows, block_count, window_rows):
    return jnp.stack(
        [
            extended[number * block_rows : number * block_rows + window_rows]
            for number in range(block_count)
        ]
    )


def phase_table(row_count, col_count, period):
    row_ids = lax.broadcasted_iota(jnp.int32, (row_count, col_count), 0)
    col_ids = lax.broadcasted_iota(jnp.int32, (row_count, col_count), 1)
    angle = (row_ids * col_ids % period).astype(wide_type) * (2.0 * math.pi / period)
    return (jnp.cos(angle), jnp.sin(angle))


def forward_dft(signal, tables):
    outer_table, cos_twist, sin_twist, forward_inner, inverse_inner = tables
    outer = jnp.einsum("kna,nmb->mkab", outer_table, signal, precision=highest)
    real_part = outer[:, 0]
    imag_part = outer[:, 1]
    twisted = jnp.stack(
        [
            real_part * cos_twist + imag_part * sin_twist,
            imag_part * cos_twist - real_part * sin_twist,
        ],
        axis=1,
    )
    return jnp.einsum("mkab,kjbq->mjaq", twisted, forward_inner, precision=highest)


def inverse_dft(spectrum, tables, total_len):
    outer_table, cos_twist, sin_twist, forward_inner, inverse_inner = tables
    inner = jnp.einsum("mkab,kjbq->mjaq", spectrum, inverse_inner, precision=highest)
    real_part = inner[:, 0]
    imag_part = inner[:, 1]
    twisted = jnp.stack(
        [
            real_part * cos_twist - imag_part * sin_twist,
            imag_part * cos_twist + real_part * sin_twist,
        ],
        axis=1,
    )
    signal = jnp.einsum("kna,mkab->nmb", outer_table, twisted, precision=highest)
    return signal / total_len


def split_wide(value):
    high = value.astype(narrow_type)
    low = (value - high.astype(wide_type)).astype(narrow_type)
    return high, low


def joined_wide(high, low):
    return high.astype(wide_type) + low.astype(wide_type)


def medium_bands(filt):
    tap_count, item_count = filt.shape
    bands = band_table(filt, tap_count, False)
    near = bands[:, :, :tap_count]
    far = jnp.concatenate(
        [bands[:, :, tap_count:], jnp.zeros((item_count, tap_count, 1), filt.dtype)], axis=2
    )
    return near, far


def channel_work(pieces, filt):
    gated_part, grad_part, gate_part, filter_part = pieces
    half_rows = gated_part.shape[0]
    chan_total = gated_part.shape[1]
    item_count = filter_part.shape[1]
    group_size = chan_total // item_count
    seq_len = half_rows * radix_cols
    full_rows = 2 * half_rows
    total_len = 2 * seq_len
    scale = 1.0 / math.sqrt(seq_len * group_size)
    by_item = (half_rows, item_count, group_size, radix_cols)
    near, far = medium_bands(filt)

    gated_items = gated_part.reshape(by_item)
    gated_prev = jnp.concatenate([jnp.zeros_like(gated_items[:1]), gated_items[:-1]], axis=0)
    mixed = (
        jnp.einsum("ngcs,gsr->ngcr", gated_items, near, preferred_element_type=wide_type)
        + jnp.einsum("ngcs,gsr->ngcr", gated_prev, far, preferred_element_type=wide_type)
    ).reshape(half_rows, chan_total, radix_cols)
    gate_wide = gate_part.astype(wide_type)
    carried = (gate_wide * mixed).astype(narrow_type)

    cos_outer, sin_outer = phase_table(half_rows, full_rows, full_rows)
    cos_twist, sin_twist = phase_table(full_rows, radix_cols, total_len)
    cos_inner, sin_inner = phase_table(radix_cols, radix_cols, radix_cols)
    outer_table = jnp.stack([cos_outer, -sin_outer])
    forward_inner = jnp.stack(
        [jnp.stack([cos_inner, -sin_inner]), jnp.stack([sin_inner, cos_inner])]
    )
    inverse_inner = jnp.stack(
        [jnp.stack([cos_inner, sin_inner]), jnp.stack([-sin_inner, cos_inner])]
    )
    tables = (outer_table, cos_twist, sin_twist, forward_inner, inverse_inner)
    shaped = (item_count, group_size, 2, full_rows, radix_cols)
    flat_shape = (chan_total, 2, full_rows, radix_cols)
    signals = jnp.concatenate([carried, grad_part], axis=1).astype(wide_type)
    both_specs = forward_dft(signals, tables)
    gated_spec = both_specs[:chan_total].reshape(shaped)
    inner_spec = both_specs[chan_total:].reshape(shaped)
    filt_spec = forward_dft(filter_part.astype(wide_type), tables)[:, None]
    gated_re = gated_spec[:, :, 0]
    gated_im = gated_spec[:, :, 1]
    inner_re = inner_spec[:, :, 0]
    inner_im = inner_spec[:, :, 1]
    filt_re = filt_spec[:, :, 0]
    filt_im = filt_spec[:, :, 1]
    conv_spec = jnp.stack(
        [gated_re * filt_re - gated_im * filt_im, gated_re * filt_im + gated_im * filt_re], axis=2
    )
    back_spec = jnp.stack(
        [inner_re * filt_re + inner_im * filt_im, inner_im * filt_re - inner_re * filt_im], axis=2
    )
    corr_spec = jnp.stack(
        [inner_re * gated_re + inner_im * gated_im, inner_im * gated_re - inner_re * gated_im],
        axis=2,
    )
    signals_back = inverse_dft(
        jnp.concatenate([conv_spec.reshape(flat_shape), back_spec.reshape(flat_shape)], axis=0),
        tables,
        total_len,
    )
    second_mix = signals_back[:, :chan_total].astype(narrow_type)
    grad_carried = signals_back[:, chan_total:].astype(narrow_type).astype(wide_type)
    summed = jnp.sum(corr_spec, axis=1)
    lagged = (inverse_dft(summed, tables, total_len) * scale).astype(narrow_type)

    grad_second = (grad_carried * mixed).astype(narrow_type)
    grad_mixed = (grad_carried * gate_wide).astype(narrow_type)
    mixed_items = grad_mixed.reshape(by_item)
    mixed_next = jnp.concatenate([mixed_items[1:], jnp.zeros_like(mixed_items[:1])], axis=0)
    grad_gated = (
        jnp.einsum("ngcs,grs->ngcr", mixed_items, near, preferred_element_type=wide_type)
        + jnp.einsum("ngcs,grs->ngcr", mixed_next, far, preferred_element_type=wide_type)
    ).reshape(half_rows, chan_total, radix_cols)
    tap_count = filt.shape[0]
    own_lags = jnp.einsum(
        "ngcs,ngcr->gsr", gated_items, mixed_items, preferred_element_type=wide_type
    )
    prev_lags = jnp.einsum(
        "ngcs,ngcr->gsr", gated_prev, mixed_items, preferred_element_type=wide_type
    )
    lag_table = jnp.concatenate([own_lags, prev_lags], axis=2).reshape(item_count, -1)
    lag_table = jnp.concatenate(
        [lag_table, jnp.zeros((item_count, tap_count), wide_type)], axis=1
    ).reshape(item_count, tap_count, 2 * tap_count + 1)
    grad_medium = jnp.sum(lag_table[:, :, :tap_count], axis=1) * scale
    squares = jnp.sum(jnp.square(lagged.astype(wide_type))) + jnp.sum(grad_medium * grad_medium)
    medium_high, medium_low = split_wide(grad_medium)
    shared = jnp.concatenate([medium_high, medium_low], axis=0)
    shared = jnp.broadcast_to(shared[None], (half_rows,) + shared.shape)
    stacked = jnp.concatenate(
        [second_mix, grad_second, grad_gated.astype(narrow_type), lagged, shared], axis=1
    )
    return stacked, squares


def body(first_gate, second_gate, output_gate, values, cotangent, medium_filter, long_filter):
    tok_rows, chan_local = first_gate.shape
    tap_count, local_groups = medium_filter.shape
    group_size = chan_local // local_groups
    ctx_devices = lax.axis_size("ctx")
    ctx_groups = local_groups // ctx_devices
    chan_share = ctx_groups * group_size
    first_wide = first_gate.astype(wide_type)
    values_wide = values.astype(wide_type)
    cotangent_wide = cotangent.astype(wide_type)
    gated_input = (first_wide * values_wide).astype(narrow_type)
    grad_inner = (cotangent_wide * output_gate.astype(wide_type)).astype(narrow_type)

    def token_major(matrix):
        return matrix.T.reshape(ctx_devices, -1, tok_rows)

    outbound = jnp.concatenate(
        [
            token_major(gated_input),
            token_major(grad_inner),
            token_major(second_gate),
            token_major(long_filter),
        ],
        axis=1,
    )
    arrived = lax.all_to_all(outbound, "ctx", 0, 0, tiled=True)
    own_filter = lax.dynamic_slice_in_dim(
        medium_filter, lax.axis_index("ctx") * ctx_groups, ctx_groups, axis=1
    )
    returned, squares = channel_work(
        (
            arrived[:, :chan_share],
            arrived[:, chan_share : 2 * chan_share],
            arrived[:, 2 * chan_share : 3 * chan_share],
            arrived[:, 3 * chan_share :],
        ),
        own_filter,
    )
    back = lax.all_to_all(returned, "ctx", 0, 0, tiled=True)

    def token_rows(start, count):
        return back[:, start : start + count].reshape(ctx_devices * count, tok_rows).T

    second_mix = token_rows(0, chan_share)
    grad_second = token_rows(chan_share, chan_share)
    grad_gated = token_rows(2 * chan_share, chan_share).astype(wide_type)
    grad_long = token_rows(3 * chan_share, ctx_groups)
    grad_medium = joined_wide(
        token_rows(3 * chan_share + ctx_groups, ctx_groups),
        token_rows(3 * chan_share + 2 * ctx_groups, ctx_groups),
    )
    every_squares = lax.all_gather(squares.reshape(1), ("ctx", "ch"), tiled=True)
    total_squares = jnp.sum(every_squares)
    grad_output_gate = (cotangent_wide * second_mix.astype(wide_type)).astype(narrow_type)
    grad_first = (grad_gated * values_wide).astype(narrow_type)
    grad_values = (grad_gated * first_wide).astype(narrow_type)
    entries = (tok_rows * ctx_devices + tap_count) * local_groups * lax.axis_size("ch")
    filter_rms = jnp.sqrt(total_squares / entries)
    return (
        grad_first,
        grad_second,
        grad_output_gate,
        grad_values,
        grad_medium,
        grad_long,
        filter_rms,
    )


def solution(mesh):
    return jax.shard_map(
        body,
        mesh=mesh,
        in_specs=(
            P("ctx", "ch"),
            P("ctx", "ch"),
            P("ctx", "ch"),
            P("ctx", "ch"),
            P("ctx", "ch"),
            P(None, "ch"),
            P("ctx", "ch"),
        ),
        out_specs=(
            P("ctx", "ch"),
            P("ctx", "ch"),
            P("ctx", "ch"),
            P("ctx", "ch"),
            P(None, "ch"),
            P("ctx", "ch"),
            P(),
        ),
        check_vma=False,
    )
```

```python
import math

import jax
import jax.numpy as jnp
from jax import lax
from jax.sharding import PartitionSpec as P

radix_cols = 128
block_limit = 64
highest = lax.Precision.HIGH
wide_type = jnp.float32
narrow_type = jnp.bfloat16


def passed_along(array, axis, by):
    peers = lax.axis_size(axis)
    pairs = [(i, i + by) for i in range(peers) if 0 <= i + by < peers]
    return lax.ppermute(array, axis, pairs)


def band_table(filt, block_rows, flipped):
    tap_count, group_count = filt.shape
    window_rows = block_rows + tap_count - 1
    leading = filt[::-1] if flipped else filt
    padded = jnp.concatenate([leading.T, jnp.zeros((group_count, block_rows), filt.dtype)], axis=1)
    tiled = jnp.broadcast_to(padded[:, None, :], (group_count, block_rows, window_rows + 1))
    tiled = tiled.reshape(group_count, block_rows * (window_rows + 1))
    return tiled[:, : block_rows * window_rows].reshape(group_count, block_rows, window_rows)


def windows_of(extended, block_rows, block_count, window_rows):
    return jnp.stack(
        [
            extended[number * block_rows : number * block_rows + window_rows]
            for number in range(block_count)
        ]
    )


def phase_table(row_count, col_count, period):
    row_ids = lax.broadcasted_iota(jnp.int32, (row_count, col_count), 0)
    col_ids = lax.broadcasted_iota(jnp.int32, (row_count, col_count), 1)
    angle = (row_ids * col_ids % period).astype(wide_type) * (2.0 * math.pi / period)
    return (jnp.cos(angle), jnp.sin(angle))


def forward_dft(signal, tables):
    outer_table, cos_twist, sin_twist, forward_inner, inverse_inner = tables
    outer = jnp.einsum("kna,nmb->mkab", outer_table, signal, precision=highest)
    real_part = outer[:, 0]
    imag_part = outer[:, 1]
    twisted = jnp.stack(
        [
            real_part * cos_twist + imag_part * sin_twist,
            imag_part * cos_twist - real_part * sin_twist,
        ],
        axis=1,
    )
    return jnp.einsum("mkab,kjbq->mjaq", twisted, forward_inner, precision=highest)


def inverse_dft(spectrum, tables, total_len):
    outer_table, cos_twist, sin_twist, forward_inner, inverse_inner = tables
    inner = jnp.einsum("mkab,kjbq->mjaq", spectrum, inverse_inner, precision=highest)
    real_part = inner[:, 0]
    imag_part = inner[:, 1]
    twisted = jnp.stack(
        [
            real_part * cos_twist - imag_part * sin_twist,
            imag_part * cos_twist + real_part * sin_twist,
        ],
        axis=1,
    )
    signal = jnp.einsum("kna,mkab->nmb", outer_table, twisted, precision=highest)
    return signal / total_len


def split_wide(value):
    high = value.astype(narrow_type)
    low = (value - high.astype(wide_type)).astype(narrow_type)
    return high, low


def joined_wide(high, low):
    return high.astype(wide_type) + low.astype(wide_type)


def medium_bands(filt):
    tap_count, item_count = filt.shape
    bands = band_table(filt, tap_count, False)
    near = bands[:, :, :tap_count]
    far = jnp.concatenate(
        [bands[:, :, tap_count:], jnp.zeros((item_count, tap_count, 1), filt.dtype)], axis=2
    )
    return near, far


def channel_work(pieces, filt):
    gated_part, grad_part, gate_part, filter_part = pieces
    half_rows = gated_part.shape[0]
    chan_total = gated_part.shape[1]
    item_count = filter_part.shape[1]
    group_size = chan_total // item_count
    seq_len = half_rows * radix_cols
    full_rows = 2 * half_rows
    total_len = 2 * seq_len
    scale = 1.0 / math.sqrt(seq_len * group_size)
    by_item = (half_rows, item_count, group_size, radix_cols)
    near, far = medium_bands(filt)

    gated_items = gated_part.reshape(by_item)
    gated_prev = jnp.concatenate([jnp.zeros_like(gated_items[:1]), gated_items[:-1]], axis=0)
    mixed = (
        jnp.einsum("ngcs,gsr->ngcr", gated_items, near, preferred_element_type=wide_type)
        + jnp.einsum("ngcs,gsr->ngcr", gated_prev, far, preferred_element_type=wide_type)
    ).reshape(half_rows, chan_total, radix_cols)
    gate_wide = gate_part.astype(wide_type)
    carried = (gate_wide * mixed).astype(narrow_type)

    cos_outer, sin_outer = phase_table(half_rows, full_rows, full_rows)
    cos_twist, sin_twist = phase_table(full_rows, radix_cols, total_len)
    cos_inner, sin_inner = phase_table(radix_cols, radix_cols, radix_cols)
    outer_table = jnp.stack([cos_outer, -sin_outer])
    forward_inner = jnp.stack(
        [jnp.stack([cos_inner, -sin_inner]), jnp.stack([sin_inner, cos_inner])]
    )
    inverse_inner = jnp.stack(
        [jnp.stack([cos_inner, sin_inner]), jnp.stack([-sin_inner, cos_inner])]
    )
    tables = (outer_table, cos_twist, sin_twist, forward_inner, inverse_inner)
    shaped = (item_count, group_size, 2, full_rows, radix_cols)
    flat_shape = (chan_total, 2, full_rows, radix_cols)
    signals = jnp.concatenate([carried, grad_part], axis=1).astype(wide_type)
    both_specs = forward_dft(signals, tables)
    gated_spec = both_specs[:chan_total].reshape(shaped)
    inner_spec = both_specs[chan_total:].reshape(shaped)
    filt_spec = forward_dft(filter_part.astype(wide_type), tables)[:, None]
    gated_re = gated_spec[:, :, 0]
    gated_im = gated_spec[:, :, 1]
    inner_re = inner_spec[:, :, 0]
    inner_im = inner_spec[:, :, 1]
    filt_re = filt_spec[:, :, 0]
    filt_im = filt_spec[:, :, 1]
    conv_spec = jnp.stack(
        [gated_re * filt_re - gated_im * filt_im, gated_re * filt_im + gated_im * filt_re], axis=2
    )
    back_spec = jnp.stack(
        [inner_re * filt_re + inner_im * filt_im, inner_im * filt_re - inner_re * filt_im], axis=2
    )
    corr_spec = jnp.stack(
        [inner_re * gated_re + inner_im * gated_im, inner_im * gated_re - inner_re * gated_im],
        axis=2,
    )
    signals_back = inverse_dft(
        jnp.concatenate([conv_spec.reshape(flat_shape), back_spec.reshape(flat_shape)], axis=0),
        tables,
        total_len,
    )
    second_mix = signals_back[:, :chan_total].astype(narrow_type)
    grad_carried = signals_back[:, chan_total:].astype(narrow_type).astype(wide_type)
    summed = jnp.sum(corr_spec, axis=1)
    lagged = (inverse_dft(summed, tables, total_len) * scale).astype(narrow_type)

    grad_second = (grad_carried * mixed).astype(narrow_type)
    grad_mixed = (grad_carried * gate_wide).astype(narrow_type)
    mixed_items = grad_mixed.reshape(by_item)
    mixed_next = jnp.concatenate([mixed_items[1:], jnp.zeros_like(mixed_items[:1])], axis=0)
    grad_gated = (
        jnp.einsum("ngcs,grs->ngcr", mixed_items, near, preferred_element_type=wide_type)
        + jnp.einsum("ngcs,grs->ngcr", mixed_next, far, preferred_element_type=wide_type)
    ).reshape(half_rows, chan_total, radix_cols)
    tap_count = filt.shape[0]
    own_lags = jnp.einsum(
        "ngcs,ngcr->gsr", gated_items, mixed_items, preferred_element_type=wide_type
    )
    prev_lags = jnp.einsum(
        "ngcs,ngcr->gsr", gated_prev, mixed_items, preferred_element_type=wide_type
    )
    lag_table = jnp.concatenate([own_lags, prev_lags], axis=2)
    lag_of = lax.broadcasted_iota(jnp.int32, (tap_count, tap_count, 2 * tap_count), 2) - (
        lax.broadcasted_iota(jnp.int32, (tap_count, tap_count, 2 * tap_count), 1)
    )
    lag_ids = lax.broadcasted_iota(jnp.int32, (tap_count, tap_count, 2 * tap_count), 0)
    on_lag = lag_of == lag_ids
    grad_medium = (
        jnp.sum(jnp.where(on_lag[None], lag_table[:, None], 0.0), axis=(2, 3)) * scale
    )
    squares = jnp.sum(jnp.square(lagged.astype(wide_type))) + jnp.sum(grad_medium * grad_medium)
    squares = lax.psum(squares, "ch")
    medium_high, medium_low = split_wide(grad_medium)
    squares_high, squares_low = split_wide(squares)
    squares_row = jnp.concatenate(
        [
            squares_high.reshape(1, 1),
            squares_low.reshape(1, 1),
            jnp.zeros((1, radix_cols - 2), narrow_type),
        ],
        axis=1,
    )
    shared = jnp.concatenate([medium_high, medium_low, squares_row], axis=0)
    shared = jnp.broadcast_to(shared[None], (half_rows,) + shared.shape)
    return jnp.concatenate(
        [second_mix, grad_second, grad_gated.astype(narrow_type), lagged, shared], axis=1
    )


def body(first_gate, second_gate, output_gate, values, cotangent, medium_filter, long_filter):
    tok_rows, chan_local = first_gate.shape
    tap_count, local_groups = medium_filter.shape
    group_size = chan_local // local_groups
    ctx_devices = lax.axis_size("ctx")
    ctx_groups = local_groups // ctx_devices
    chan_share = ctx_groups * group_size
    first_wide = first_gate.astype(wide_type)
    values_wide = values.astype(wide_type)
    cotangent_wide = cotangent.astype(wide_type)
    gated_input = (first_wide * values_wide).astype(narrow_type)
    grad_inner = (cotangent_wide * output_gate.astype(wide_type)).astype(narrow_type)

    def token_major(matrix):
        return matrix.T.reshape(ctx_devices, -1, tok_rows)

    outbound = jnp.concatenate(
        [
            token_major(gated_input),
            token_major(grad_inner),
            token_major(second_gate),
            token_major(long_filter),
        ],
        axis=1,
    )
    arrived = lax.all_to_all(outbound, "ctx", 0, 0, tiled=True)
    own_filter = lax.dynamic_slice_in_dim(
        medium_filter, lax.axis_index("ctx") * ctx_groups, ctx_groups, axis=1
    )
    returned = channel_work(
        (
            arrived[:, :chan_share],
            arrived[:, chan_share : 2 * chan_share],
            arrived[:, 2 * chan_share : 3 * chan_share],
            arrived[:, 3 * chan_share :],
        ),
        own_filter,
    )
    back = lax.all_to_all(returned, "ctx", 0, 0, tiled=True)

    def token_rows(start, count):
        return back[:, start : start + count].reshape(ctx_devices * count, tok_rows).T

    second_mix = token_rows(0, chan_share)
    grad_second = token_rows(chan_share, chan_share)
    grad_gated = token_rows(2 * chan_share, chan_share).astype(wide_type)
    grad_long = token_rows(3 * chan_share, ctx_groups)
    grad_medium = joined_wide(
        token_rows(3 * chan_share + ctx_groups, ctx_groups),
        token_rows(3 * chan_share + 2 * ctx_groups, ctx_groups),
    )
    squares_row = back[:, 3 * chan_share + 3 * ctx_groups]
    total_squares = jnp.sum(joined_wide(squares_row[:, 0], squares_row[:, 1]))
    grad_output_gate = (cotangent_wide * second_mix.astype(wide_type)).astype(narrow_type)
    grad_first = (grad_gated * values_wide).astype(narrow_type)
    grad_values = (grad_gated * first_wide).astype(narrow_type)
    entries = (tok_rows * ctx_devices + tap_count) * local_groups * lax.axis_size("ch")
    filter_rms = jnp.sqrt(total_squares / entries)
    return (
        grad_first,
        grad_second,
        grad_output_gate,
        grad_values,
        grad_medium,
        grad_long,
        filter_rms,
    )


def solution(mesh):
    return jax.shard_map(
        body,
        mesh=mesh,
        in_specs=(
            P("ctx", "ch"),
            P("ctx", "ch"),
            P("ctx", "ch"),
            P("ctx", "ch"),
            P("ctx", "ch"),
            P(None, "ch"),
            P("ctx", "ch"),
        ),
        out_specs=(
            P("ctx", "ch"),
            P("ctx", "ch"),
            P("ctx", "ch"),
            P("ctx", "ch"),
            P(None, "ch"),
            P("ctx", "ch"),
            P(),
        ),
        check_vma=False,
    )
```

```python
import math

import jax
import jax.numpy as jnp
from jax import lax
from jax.sharding import PartitionSpec as P

radix_cols = 128
block_limit = 64
highest = lax.Precision.HIGH
wide_type = jnp.float32
narrow_type = jnp.bfloat16


def passed_along(array, axis, by):
    peers = lax.axis_size(axis)
    pairs = [(i, i + by) for i in range(peers) if 0 <= i + by < peers]
    return lax.ppermute(array, axis, pairs)


def band_table(filt, block_rows, flipped):
    tap_count, group_count = filt.shape
    window_rows = block_rows + tap_count - 1
    leading = filt[::-1] if flipped else filt
    padded = jnp.concatenate([leading.T, jnp.zeros((group_count, block_rows), filt.dtype)], axis=1)
    tiled = jnp.broadcast_to(padded[:, None, :], (group_count, block_rows, window_rows + 1))
    tiled = tiled.reshape(group_count, block_rows * (window_rows + 1))
    return tiled[:, : block_rows * window_rows].reshape(group_count, block_rows, window_rows)


def windows_of(extended, block_rows, block_count, window_rows):
    return jnp.stack(
        [
            extended[number * block_rows : number * block_rows + window_rows]
            for number in range(block_count)
        ]
    )


def phase_table(row_count, col_count, period):
    row_ids = lax.broadcasted_iota(jnp.int32, (row_count, col_count), 0)
    col_ids = lax.broadcasted_iota(jnp.int32, (row_count, col_count), 1)
    angle = (row_ids * col_ids % period).astype(wide_type) * (2.0 * math.pi / period)
    return (jnp.cos(angle), jnp.sin(angle))


def forward_dft(signal, tables):
    outer_table, cos_twist, sin_twist, forward_inner, inverse_inner = tables
    outer = jnp.einsum("kna,nmb->mkab", outer_table, signal, precision=highest)
    real_part = outer[:, 0]
    imag_part = outer[:, 1]
    twisted = jnp.stack(
        [
            real_part * cos_twist + imag_part * sin_twist,
            imag_part * cos_twist - real_part * sin_twist,
        ],
        axis=1,
    )
    return jnp.einsum("mkab,kjbq->mjaq", twisted, forward_inner, precision=highest)


def inverse_dft(spectrum, tables, total_len):
    outer_table, cos_twist, sin_twist, forward_inner, inverse_inner = tables
    inner = jnp.einsum("mkab,kjbq->mjaq", spectrum, inverse_inner, precision=highest)
    real_part = inner[:, 0]
    imag_part = inner[:, 1]
    twisted = jnp.stack(
        [
            real_part * cos_twist - imag_part * sin_twist,
            imag_part * cos_twist + real_part * sin_twist,
        ],
        axis=1,
    )
    signal = jnp.einsum("kna,mkab->nmb", outer_table, twisted, precision=highest)
    return signal / total_len


def split_wide(value):
    high = value.astype(narrow_type)
    low = (value - high.astype(wide_type)).astype(narrow_type)
    return high, low


def joined_wide(high, low):
    return high.astype(wide_type) + low.astype(wide_type)


def medium_bands(filt):
    tap_count, item_count = filt.shape
    bands = band_table(filt, tap_count, False)
    near = bands[:, :, :tap_count]
    far = jnp.concatenate(
        [bands[:, :, tap_count:], jnp.zeros((item_count, tap_count, 1), filt.dtype)], axis=2
    )
    return near, far


def channel_work(pieces, filt):
    gated_part, grad_part, gate_part, filter_part = pieces
    half_rows = gated_part.shape[0]
    chan_total = gated_part.shape[1]
    item_count = filter_part.shape[1]
    group_size = chan_total // item_count
    seq_len = half_rows * radix_cols
    full_rows = 2 * half_rows
    total_len = 2 * seq_len
    scale = 1.0 / math.sqrt(seq_len * group_size)
    by_item = (half_rows, item_count, group_size, radix_cols)
    near, far = medium_bands(filt)

    gated_items = gated_part.reshape(by_item)
    gated_prev = jnp.concatenate([jnp.zeros_like(gated_items[:1]), gated_items[:-1]], axis=0)
    mixed = (
        jnp.einsum("ngcs,gsr->ngcr", gated_items, near, preferred_element_type=wide_type)
        + jnp.einsum("ngcs,gsr->ngcr", gated_prev, far, preferred_element_type=wide_type)
    ).reshape(half_rows, chan_total, radix_cols)
    gate_wide = gate_part.astype(wide_type)
    carried = (gate_wide * mixed).astype(narrow_type)

    cos_outer, sin_outer = phase_table(half_rows, full_rows, full_rows)
    cos_twist, sin_twist = phase_table(full_rows, radix_cols, total_len)
    cos_inner, sin_inner = phase_table(radix_cols, radix_cols, radix_cols)
    outer_table = jnp.stack([cos_outer, -sin_outer])
    forward_inner = jnp.stack(
        [jnp.stack([cos_inner, -sin_inner]), jnp.stack([sin_inner, cos_inner])]
    )
    inverse_inner = jnp.stack(
        [jnp.stack([cos_inner, sin_inner]), jnp.stack([-sin_inner, cos_inner])]
    )
    tables = (outer_table, cos_twist, sin_twist, forward_inner, inverse_inner)
    shaped = (item_count, group_size, 2, full_rows, radix_cols)
    flat_shape = (chan_total, 2, full_rows, radix_cols)
    signals = jnp.concatenate([carried, grad_part], axis=1).astype(wide_type)
    both_specs = forward_dft(signals, tables)
    gated_spec = both_specs[:chan_total].reshape(shaped)
    inner_spec = both_specs[chan_total:].reshape(shaped)
    filt_spec = forward_dft(filter_part.astype(wide_type), tables)[:, None]
    gated_re = gated_spec[:, :, 0]
    gated_im = gated_spec[:, :, 1]
    inner_re = inner_spec[:, :, 0]
    inner_im = inner_spec[:, :, 1]
    filt_re = filt_spec[:, :, 0]
    filt_im = filt_spec[:, :, 1]
    conv_spec = jnp.stack(
        [gated_re * filt_re - gated_im * filt_im, gated_re * filt_im + gated_im * filt_re], axis=2
    )
    back_spec = jnp.stack(
        [inner_re * filt_re + inner_im * filt_im, inner_im * filt_re - inner_re * filt_im], axis=2
    )
    corr_spec = jnp.stack(
        [inner_re * gated_re + inner_im * gated_im, inner_im * gated_re - inner_re * gated_im],
        axis=2,
    )
    signals_back = inverse_dft(
        jnp.concatenate([conv_spec.reshape(flat_shape), back_spec.reshape(flat_shape)], axis=0),
        tables,
        total_len,
    )
    second_mix = signals_back[:, :chan_total].astype(narrow_type)
    grad_carried = signals_back[:, chan_total:].astype(narrow_type).astype(wide_type)
    summed = jnp.sum(corr_spec, axis=1)
    lagged = (inverse_dft(summed, tables, total_len) * scale).astype(narrow_type)

    grad_second = (grad_carried * mixed).astype(narrow_type)
    grad_mixed = (grad_carried * gate_wide).astype(narrow_type)
    mixed_items = grad_mixed.reshape(by_item)
    mixed_next = jnp.concatenate([mixed_items[1:], jnp.zeros_like(mixed_items[:1])], axis=0)
    grad_gated = (
        jnp.einsum("ngcs,grs->ngcr", mixed_items, near, preferred_element_type=wide_type)
        + jnp.einsum("ngcs,grs->ngcr", mixed_next, far, preferred_element_type=wide_type)
    ).reshape(half_rows, chan_total, radix_cols)
    tap_count = filt.shape[0]
    own_lags = jnp.einsum(
        "ngcs,ngcr->gsr", gated_items, mixed_items, preferred_element_type=wide_type
    )
    prev_lags = jnp.einsum(
        "ngcs,ngcr->gsr", gated_prev, mixed_items, preferred_element_type=wide_type
    )
    cube = (tap_count, tap_count, tap_count)
    lag_of = lax.broadcasted_iota(jnp.int32, cube, 2) - lax.broadcasted_iota(jnp.int32, cube, 1)
    lag_ids = lax.broadcasted_iota(jnp.int32, cube, 0)
    on_own = (lag_of == lag_ids)[None]
    on_prev = (lag_of + tap_count == lag_ids)[None]
    grad_medium = (
        jnp.sum(
            jnp.where(on_own, own_lags[:, None], 0.0) + jnp.where(on_prev, prev_lags[:, None], 0.0),
            axis=(2, 3),
        )
        * scale
    )
    squares = jnp.sum(jnp.square(lagged.astype(wide_type))) + jnp.sum(grad_medium * grad_medium)
    squares = lax.psum(squares, "ch")
    medium_high, medium_low = split_wide(grad_medium)
    squares_high, squares_low = split_wide(squares)
    squares_row = jnp.concatenate(
        [
            squares_high.reshape(1, 1),
            squares_low.reshape(1, 1),
            jnp.zeros((1, radix_cols - 2), narrow_type),
        ],
        axis=1,
    )
    shared = jnp.concatenate([medium_high, medium_low, squares_row], axis=0)
    shared = jnp.broadcast_to(shared[None], (half_rows,) + shared.shape)
    return jnp.concatenate(
        [second_mix, grad_second, grad_gated.astype(narrow_type), lagged, shared], axis=1
    )


def body(first_gate, second_gate, output_gate, values, cotangent, medium_filter, long_filter):
    tok_rows, chan_local = first_gate.shape
    tap_count, local_groups = medium_filter.shape
    group_size = chan_local // local_groups
    ctx_devices = lax.axis_size("ctx")
    ctx_groups = local_groups // ctx_devices
    chan_share = ctx_groups * group_size
    first_wide = first_gate.astype(wide_type)
    values_wide = values.astype(wide_type)
    cotangent_wide = cotangent.astype(wide_type)
    gated_input = (first_wide * values_wide).astype(narrow_type)
    grad_inner = (cotangent_wide * output_gate.astype(wide_type)).astype(narrow_type)

    def token_major(matrix):
        return matrix.T.reshape(ctx_devices, -1, tok_rows)

    outbound = jnp.concatenate(
        [
            token_major(gated_input),
            token_major(grad_inner),
            token_major(second_gate),
            token_major(long_filter),
        ],
        axis=1,
    )
    arrived = lax.all_to_all(outbound, "ctx", 0, 0, tiled=True)
    own_filter = lax.dynamic_slice_in_dim(
        medium_filter, lax.axis_index("ctx") * ctx_groups, ctx_groups, axis=1
    )
    returned = channel_work(
        (
            arrived[:, :chan_share],
            arrived[:, chan_share : 2 * chan_share],
            arrived[:, 2 * chan_share : 3 * chan_share],
            arrived[:, 3 * chan_share :],
        ),
        own_filter,
    )
    back = lax.all_to_all(returned, "ctx", 0, 0, tiled=True)

    def token_rows(start, count):
        return back[:, start : start + count].reshape(ctx_devices * count, tok_rows).T

    second_mix = token_rows(0, chan_share)
    grad_second = token_rows(chan_share, chan_share)
    grad_gated = token_rows(2 * chan_share, chan_share).astype(wide_type)
    grad_long = token_rows(3 * chan_share, ctx_groups)
    grad_medium = joined_wide(
        token_rows(3 * chan_share + ctx_groups, ctx_groups),
        token_rows(3 * chan_share + 2 * ctx_groups, ctx_groups),
    )
    squares_row = back[:, 3 * chan_share + 3 * ctx_groups]
    total_squares = jnp.sum(joined_wide(squares_row[:, 0], squares_row[:, 1]))
    grad_output_gate = (cotangent_wide * second_mix.astype(wide_type)).astype(narrow_type)
    grad_first = (grad_gated * values_wide).astype(narrow_type)
    grad_values = (grad_gated * first_wide).astype(narrow_type)
    entries = (tok_rows * ctx_devices + tap_count) * local_groups * lax.axis_size("ch")
    filter_rms = jnp.sqrt(total_squares / entries)
    return (
        grad_first,
        grad_second,
        grad_output_gate,
        grad_values,
        grad_medium,
        grad_long,
        filter_rms,
    )


def solution(mesh):
    return jax.shard_map(
        body,
        mesh=mesh,
        in_specs=(
            P("ctx", "ch"),
            P("ctx", "ch"),
            P("ctx", "ch"),
            P("ctx", "ch"),
            P("ctx", "ch"),
            P(None, "ch"),
            P("ctx", "ch"),
        ),
        out_specs=(
            P("ctx", "ch"),
            P("ctx", "ch"),
            P("ctx", "ch"),
            P("ctx", "ch"),
            P(None, "ch"),
            P("ctx", "ch"),
            P(),
        ),
        check_vma=False,
    )
```

```python
import math

import jax
import jax.numpy as jnp
from jax import lax
from jax.sharding import PartitionSpec as P

radix_cols = 128
block_limit = 64
highest = lax.Precision.HIGH
wide_type = jnp.float32
narrow_type = jnp.bfloat16


def passed_along(array, axis, by):
    peers = lax.axis_size(axis)
    pairs = [(i, i + by) for i in range(peers) if 0 <= i + by < peers]
    return lax.ppermute(array, axis, pairs)


def band_table(filt, block_rows, flipped):
    tap_count, group_count = filt.shape
    window_rows = block_rows + tap_count - 1
    leading = filt[::-1] if flipped else filt
    padded = jnp.concatenate([leading.T, jnp.zeros((group_count, block_rows), filt.dtype)], axis=1)
    tiled = jnp.broadcast_to(padded[:, None, :], (group_count, block_rows, window_rows + 1))
    tiled = tiled.reshape(group_count, block_rows * (window_rows + 1))
    return tiled[:, : block_rows * window_rows].reshape(group_count, block_rows, window_rows)


def windows_of(extended, block_rows, block_count, window_rows):
    return jnp.stack(
        [
            extended[number * block_rows : number * block_rows + window_rows]
            for number in range(block_count)
        ]
    )


def phase_table(row_count, col_count, period):
    row_ids = lax.broadcasted_iota(jnp.int32, (row_count, col_count), 0)
    col_ids = lax.broadcasted_iota(jnp.int32, (row_count, col_count), 1)
    angle = (row_ids * col_ids % period).astype(wide_type) * (2.0 * math.pi / period)
    return (jnp.cos(angle), jnp.sin(angle))


def forward_dft(signal, tables):
    outer_table, cos_twist, sin_twist, forward_inner, inverse_inner = tables
    outer = jnp.einsum("kna,nmb->mkab", outer_table, signal, precision=highest)
    real_part = outer[:, 0]
    imag_part = outer[:, 1]
    twisted = jnp.stack(
        [
            real_part * cos_twist + imag_part * sin_twist,
            imag_part * cos_twist - real_part * sin_twist,
        ],
        axis=1,
    )
    return jnp.einsum("mkab,kjbq->mjaq", twisted, forward_inner, precision=highest)


def inverse_dft(spectrum, tables, total_len):
    outer_table, cos_twist, sin_twist, forward_inner, inverse_inner = tables
    inner = jnp.einsum("mkab,kjbq->mjaq", spectrum, inverse_inner, precision=highest)
    real_part = inner[:, 0]
    imag_part = inner[:, 1]
    twisted = jnp.stack(
        [
            real_part * cos_twist - imag_part * sin_twist,
            imag_part * cos_twist + real_part * sin_twist,
        ],
        axis=1,
    )
    signal = jnp.einsum("kna,mkab->nmb", outer_table, twisted, precision=highest)
    return signal / total_len


def split_wide(value):
    high = value.astype(narrow_type)
    low = (value - high.astype(wide_type)).astype(narrow_type)
    return high, low


def joined_wide(high, low):
    return high.astype(wide_type) + low.astype(wide_type)


def medium_bands(filt):
    tap_count, item_count = filt.shape
    bands = band_table(filt, tap_count, False)
    near = bands[:, :, :tap_count]
    far = jnp.concatenate(
        [bands[:, :, tap_count:], jnp.zeros((item_count, tap_count, 1), filt.dtype)], axis=2
    )
    return near, far


def channel_work(pieces, filt):
    gated_part, grad_part, gate_part, filter_part = pieces
    half_rows = gated_part.shape[0]
    chan_total = gated_part.shape[1]
    item_count = filter_part.shape[1]
    group_size = chan_total // item_count
    seq_len = half_rows * radix_cols
    full_rows = 2 * half_rows
    total_len = 2 * seq_len
    scale = 1.0 / math.sqrt(seq_len * group_size)
    by_item = (half_rows, item_count, group_size, radix_cols)
    near, far = medium_bands(filt)

    gated_items = gated_part.reshape(by_item)
    gated_prev = jnp.concatenate([jnp.zeros_like(gated_items[:1]), gated_items[:-1]], axis=0)
    mixed = jnp.einsum(
        "ngcs,gsr->ngcr",
        jnp.concatenate([gated_items, gated_prev], axis=3),
        jnp.concatenate([near, far], axis=1),
        preferred_element_type=wide_type,
    ).reshape(half_rows, chan_total, radix_cols)
    gate_wide = gate_part.astype(wide_type)
    carried = (gate_wide * mixed).astype(narrow_type)

    cos_outer, sin_outer = phase_table(half_rows, full_rows, full_rows)
    cos_twist, sin_twist = phase_table(full_rows, radix_cols, total_len)
    cos_inner, sin_inner = phase_table(radix_cols, radix_cols, radix_cols)
    outer_table = jnp.stack([cos_outer, -sin_outer])
    forward_inner = jnp.stack(
        [jnp.stack([cos_inner, -sin_inner]), jnp.stack([sin_inner, cos_inner])]
    )
    inverse_inner = jnp.stack(
        [jnp.stack([cos_inner, sin_inner]), jnp.stack([-sin_inner, cos_inner])]
    )
    tables = (outer_table, cos_twist, sin_twist, forward_inner, inverse_inner)
    shaped = (item_count, group_size, 2, full_rows, radix_cols)
    flat_shape = (chan_total, 2, full_rows, radix_cols)
    signals = jnp.concatenate([carried, grad_part], axis=1).astype(wide_type)
    both_specs = forward_dft(signals, tables)
    gated_spec = both_specs[:chan_total].reshape(shaped)
    inner_spec = both_specs[chan_total:].reshape(shaped)
    filt_spec = forward_dft(filter_part.astype(wide_type), tables)[:, None]
    gated_re = gated_spec[:, :, 0]
    gated_im = gated_spec[:, :, 1]
    inner_re = inner_spec[:, :, 0]
    inner_im = inner_spec[:, :, 1]
    filt_re = filt_spec[:, :, 0]
    filt_im = filt_spec[:, :, 1]
    conv_spec = jnp.stack(
        [gated_re * filt_re - gated_im * filt_im, gated_re * filt_im + gated_im * filt_re], axis=2
    )
    back_spec = jnp.stack(
        [inner_re * filt_re + inner_im * filt_im, inner_im * filt_re - inner_re * filt_im], axis=2
    )
    corr_spec = jnp.stack(
        [inner_re * gated_re + inner_im * gated_im, inner_im * gated_re - inner_re * gated_im],
        axis=2,
    )
    signals_back = inverse_dft(
        jnp.concatenate([conv_spec.reshape(flat_shape), back_spec.reshape(flat_shape)], axis=0),
        tables,
        total_len,
    )
    second_mix = signals_back[:, :chan_total].astype(narrow_type)
    grad_carried = signals_back[:, chan_total:].astype(narrow_type).astype(wide_type)
    summed = jnp.sum(corr_spec, axis=1)
    lagged = (inverse_dft(summed, tables, total_len) * scale).astype(narrow_type)

    grad_second = (grad_carried * mixed).astype(narrow_type)
    grad_mixed = (grad_carried * gate_wide).astype(narrow_type)
    mixed_items = grad_mixed.reshape(by_item)
    mixed_next = jnp.concatenate([mixed_items[1:], jnp.zeros_like(mixed_items[:1])], axis=0)
    grad_gated = jnp.einsum(
        "ngcs,grs->ngcr",
        jnp.concatenate([mixed_items, mixed_next], axis=3),
        jnp.concatenate([near, far], axis=2),
        preferred_element_type=wide_type,
    ).reshape(half_rows, chan_total, radix_cols)
    tap_count = filt.shape[0]
    own_lags = jnp.einsum(
        "ngcs,ngcr->gsr", gated_items, mixed_items, preferred_element_type=wide_type
    )
    prev_lags = jnp.einsum(
        "ngcs,ngcr->gsr", gated_prev, mixed_items, preferred_element_type=wide_type
    )
    cube = (tap_count, tap_count, tap_count)
    lag_of = lax.broadcasted_iota(jnp.int32, cube, 2) - lax.broadcasted_iota(jnp.int32, cube, 1)
    lag_ids = lax.broadcasted_iota(jnp.int32, cube, 0)
    on_own = (lag_of == lag_ids)[None]
    on_prev = (lag_of + tap_count == lag_ids)[None]
    grad_medium = (
        jnp.sum(
            jnp.where(on_own, own_lags[:, None], 0.0) + jnp.where(on_prev, prev_lags[:, None], 0.0),
            axis=(2, 3),
        )
        * scale
    )
    squares = jnp.sum(jnp.square(lagged.astype(wide_type))) + jnp.sum(grad_medium * grad_medium)
    squares = lax.psum(squares, "ch")
    medium_high, medium_low = split_wide(grad_medium)
    squares_high, squares_low = split_wide(squares)
    squares_row = jnp.concatenate(
        [
            squares_high.reshape(1, 1),
            squares_low.reshape(1, 1),
            jnp.zeros((1, radix_cols - 2), narrow_type),
        ],
        axis=1,
    )
    shared = jnp.concatenate([medium_high, medium_low, squares_row], axis=0)
    shared = jnp.broadcast_to(shared[None], (half_rows,) + shared.shape)
    return jnp.concatenate(
        [second_mix, grad_second, grad_gated.astype(narrow_type), lagged, shared], axis=1
    )


def body(first_gate, second_gate, output_gate, values, cotangent, medium_filter, long_filter):
    tok_rows, chan_local = first_gate.shape
    tap_count, local_groups = medium_filter.shape
    group_size = chan_local // local_groups
    ctx_devices = lax.axis_size("ctx")
    ctx_groups = local_groups // ctx_devices
    chan_share = ctx_groups * group_size
    first_wide = first_gate.astype(wide_type)
    values_wide = values.astype(wide_type)
    cotangent_wide = cotangent.astype(wide_type)
    gated_input = (first_wide * values_wide).astype(narrow_type)
    grad_inner = (cotangent_wide * output_gate.astype(wide_type)).astype(narrow_type)

    def token_major(matrix):
        return matrix.T.reshape(ctx_devices, -1, tok_rows)

    streams = jnp.stack([gated_input, grad_inner, second_gate])
    streams = streams.reshape(3, tok_rows, ctx_devices, chan_share).transpose(2, 0, 3, 1)
    outbound = jnp.concatenate(
        [streams.reshape(ctx_devices, 3 * chan_share, tok_rows), token_major(long_filter)],
        axis=1,
    )
    arrived = lax.all_to_all(outbound, "ctx", 0, 0, tiled=True)
    own_filter = lax.dynamic_slice_in_dim(
        medium_filter, lax.axis_index("ctx") * ctx_groups, ctx_groups, axis=1
    )
    returned = channel_work(
        (
            arrived[:, :chan_share],
            arrived[:, chan_share : 2 * chan_share],
            arrived[:, 2 * chan_share : 3 * chan_share],
            arrived[:, 3 * chan_share :],
        ),
        own_filter,
    )
    back = lax.all_to_all(returned, "ctx", 0, 0, tiled=True)

    def token_rows(start, count):
        return back[:, start : start + count].reshape(ctx_devices * count, tok_rows).T

    second_mix = token_rows(0, chan_share)
    grad_second = token_rows(chan_share, chan_share)
    grad_gated = token_rows(2 * chan_share, chan_share).astype(wide_type)
    grad_long = token_rows(3 * chan_share, ctx_groups)
    grad_medium = joined_wide(
        token_rows(3 * chan_share + ctx_groups, ctx_groups),
        token_rows(3 * chan_share + 2 * ctx_groups, ctx_groups),
    )
    squares_row = back[:, 3 * chan_share + 3 * ctx_groups]
    total_squares = jnp.sum(joined_wide(squares_row[:, 0], squares_row[:, 1]))
    grad_output_gate = (cotangent_wide * second_mix.astype(wide_type)).astype(narrow_type)
    grad_first = (grad_gated * values_wide).astype(narrow_type)
    grad_values = (grad_gated * first_wide).astype(narrow_type)
    entries = (tok_rows * ctx_devices + tap_count) * local_groups * lax.axis_size("ch")
    filter_rms = jnp.sqrt(total_squares / entries)
    return (
        grad_first,
        grad_second,
        grad_output_gate,
        grad_values,
        grad_medium,
        grad_long,
        filter_rms,
    )


def solution(mesh):
    return jax.shard_map(
        body,
        mesh=mesh,
        in_specs=(
            P("ctx", "ch"),
            P("ctx", "ch"),
            P("ctx", "ch"),
            P("ctx", "ch"),
            P("ctx", "ch"),
            P(None, "ch"),
            P("ctx", "ch"),
        ),
        out_specs=(
            P("ctx", "ch"),
            P("ctx", "ch"),
            P("ctx", "ch"),
            P("ctx", "ch"),
            P(None, "ch"),
            P("ctx", "ch"),
            P(),
        ),
        check_vma=False,
    )
```
